32 devices in a mesh: dp: 4 (over y, core), freq: 8 (over z, x).
Axes of the slice: x: 2, y: 2, z: 4, core: 2. Of those that a mesh axis runs over, the one named last changes fastest.
Arguments:
- grad_parts: float32 [4, 27, 4, 65536], P('dp', None, None, 'freq'), may hold values from -12 to 12
- kernel: float32 [27, 262144], P(None, ('dp', 'freq')), may hold values from -4 to 4
Outputs:
- clipped: float32 [27, 262144], P(None, ('dp', 'freq'))
The draws below stay inside these ranges and needn't reach their ends.
All inputs are finite; a program needn't handle non-finite values.
Results may differ from the reference program's by a relative error of at most 0.0005.
The reference program's roundings to bfloat16 on the way count: a program that leaves them out, or rounds other values in their place, can miss the bound.
Values may be sent and summed in bfloat16 or wider, within the bound.
No kernel may reach another device: no remote copies, remote signals or barrier semaphores. Data moves between devices by JAX's collectives and lax.ppermute only.
A program may use at most 64 MiB of HBM per device.

```python
import math
import jax
import jax.numpy as jnp
from jax import lax

C = 512
TAPS = 27
GT = 8
GH = 32
GW = 32
K = 64
STRIDE = 128
N_DP = 4


def draw_grad_parts(key, part):
    width = C * C // N_DP
    key_noise = jax.random.fold_in(key, 11)
    key_shared = jax.random.fold_in(key, 12)
    key_pairing = jax.random.fold_in(key, 13)
    pairing = jax.random.permutation(key_pairing, jnp.arange(N_DP, dtype=jnp.int32))
    blocks = jnp.arange(N_DP, dtype=jnp.int32)
    spike = jnp.where(pairing[:, None, None, None] == blocks[None, None, :, None], 3.0, 1.0).astype(jnp.float32)
    noise = jnp.clip(jax.random.normal(key_noise, (N_DP, TAPS, N_DP, width), jnp.float32), -3.0, 3.0)
    shared = jnp.clip(jax.random.normal(key_shared, (1, TAPS, N_DP, width), jnp.float32), -3.0, 3.0)
    return jnp.clip(spike * noise + shared, -12.0, 12.0).astype(jnp.float32)


def shard_levels(key, shape, shards, least, largest):
    factor_of = 1.0
    for axis_at, parts in shards:
        heights = jax.random.uniform(jax.random.fold_in(jax.random.fold_in(key, 6), axis_at), (parts,), jnp.float32, least / len(shards), largest / len(shards))
        factor_of = factor_of * jnp.repeat(jnp.exp(heights), shape[axis_at] // parts).reshape((-1,) + (1,) * (len(shape) - 1 - axis_at))
    return factor_of


def centred(stream_key, extent, deviation, bound, cuts=(), kind=jnp.bfloat16):
    array = deviation * jax.random.normal(stream_key, extent, jnp.float32)
    if cuts:
        array = array * shard_levels(stream_key, extent, cuts, -0.22, 0.18)
    return jnp.clip(array, -bound, bound).astype(kind)


def setup_inputs(seed: int = 0) -> dict:
    splits = jax.random.split(jax.random.key(seed), 3)
    grad_parts = draw_grad_parts(jax.random.fold_in(splits[2], 71), 0)
    kernel = centred(splits[1], (TAPS, C * C), 0.25, 4.0, ((1, 32),), jnp.float32)
    return {"grad_parts": grad_parts, "kernel": kernel}


CLIP = 0.25
HIGH = lax.Precision.HIGHEST

def tap_phases(freq_ids, stride):
    flat_index = freq_ids * stride
    freq_time = flat_index // (GH * GW)
    freq_row = flat_index // GW % GH
    freq_col = flat_index % GW
    taps = jnp.arange(TAPS, dtype=jnp.int32)
    off_time = taps // 9 - 1
    off_row = taps // 3 % 3 - 1
    off_col = taps % 3 - 1
    period = GT * GH * GW
    turns = (freq_time[:, None] * off_time[None, :] * (GH * GW) + freq_row[:, None] * off_row[None, :] * (GT * GW) + freq_col[:, None] * off_col[None, :] * (GT * GH)) % period
    angle = turns.astype(jnp.float32) * (2.0 * math.pi / period)
    return (jnp.cos(angle), jnp.sin(angle))

def polar_step(spectra):
    width = spectra.shape[-1]
    values = spectra.astype(jnp.float32)
    mean_square = lax.optimization_barrier(jnp.mean(values * values, axis=(1, 2, 3), keepdims=True))
    spread = math.sqrt(8.0 * width)
    scaled = (values * (0.75 / (spread * jnp.sqrt(mean_square + 1e-06)))).astype(jnp.bfloat16).astype(jnp.float32)
    real_part = scaled[:, 0]
    imag_part = scaled[:, 1]
    stacked = jnp.concatenate([real_part, imag_part], axis=1)
    turned = jnp.concatenate([imag_part, -real_part], axis=1)
    gram = jnp.einsum('nri,nrj->nij', stacked, jnp.concatenate([stacked, turned], axis=2), precision=HIGH)
    gram = gram.astype(jnp.bfloat16).astype(jnp.float32)
    gram_real = gram[:, :, :width]
    gram_imag = gram[:, :, width:]
    blocked = jnp.concatenate([gram, jnp.concatenate([-gram_imag, gram_real], axis=2)], axis=1)
    side = jnp.concatenate([real_part, imag_part], axis=2)
    product = jnp.einsum('nij,njk->nik', side, blocked, precision=HIGH)
    result = (1.5 * side - 0.5 * product).astype(jnp.bfloat16)
    return jnp.stack([result[:, :, :width], result[:, :, width:]], axis=1)

def reference(grad_parts, kernel):
    gradient = lax.optimization_barrier(jnp.sum(grad_parts, axis=0)).reshape(TAPS, C * C)
    norm_value = jnp.sqrt(jnp.sum(gradient * gradient) + 1e-06)
    factor = jnp.minimum(1.0, CLIP * math.sqrt(TAPS * C * C) / norm_value)
    flat = kernel - factor * gradient
    block_size = 8
    freq_blocks = jnp.arange(K, dtype=jnp.int32).reshape(K // block_size, block_size)

    def one_block(summed, freq_ids):
        cosine, sine_rows = tap_phases(freq_ids, STRIDE)
        real_spec = jnp.dot(cosine, flat, precision=HIGH)
        imag_spec = -jnp.dot(sine_rows, flat, precision=HIGH)
        spectra = jnp.stack([real_spec, imag_spec], axis=1).reshape(block_size, 2, C, C).astype(jnp.bfloat16)
        polar_part = polar_step(spectra).astype(jnp.float32)
        summed = summed + jnp.dot(cosine.T, polar_part[:, 0].reshape(block_size, C * C), precision=HIGH)
        summed = summed - jnp.dot(sine_rows.T, polar_part[:, 1].reshape(block_size, C * C), precision=HIGH)
        return (summed, None)
    summed, _ = lax.scan(one_block, jnp.zeros((TAPS, C * C), jnp.float32), freq_blocks)
    return summed * math.sqrt(C / K)
```

```python
import math

import numpy as np

import jax
import jax.numpy as jnp
from jax import lax
from jax.sharding import PartitionSpec as P

C = 512
TAPS = 27
GT = 8
GH = 32
GW = 32
KD = 2

CLIP = 0.25
HIGH = lax.Precision.HIGHEST
AXES = ("dp", "freq")


def grid_point(freq_ids, stride):
    flat_index = freq_ids * stride
    return flat_index // (GH * GW), flat_index // GW % GH, flat_index % GW


def turns_of(freq_ids, stride):
    freq_time, freq_row, freq_col = grid_point(freq_ids, stride)
    taps = np.arange(TAPS)
    off_time = taps // 9 - 1
    off_row = taps // 3 % 3 - 1
    off_col = taps % 3 - 1
    period = GT * GH * GW
    return (
        freq_time[:, None] * off_time[None, :] * (GH * GW)
        + freq_row[:, None] * off_row[None, :] * (GT * GW)
        + freq_col[:, None] * off_col[None, :] * (GT * GH)
    ) % period


def slot_plan(total_freq, stride):
    ids = np.arange(total_freq)
    freq_time, freq_row, freq_col = grid_point(ids, stride)
    key = {(int(a), int(b), int(c)): j for j, (a, b, c) in enumerate(zip(freq_time, freq_row, freq_col))}
    pairs, selfs, seen = [], [], set()
    for j in range(total_freq):
        if j in seen:
            continue
        mate = key[(int(-freq_time[j] % GT), int(-freq_row[j] % GH), int(-freq_col[j] % GW))]
        seen.update((j, mate))
        if mate == j:
            selfs.append(j)
        else:
            pairs.append(j)
    assert len(selfs) % 2 == 0
    period = GT * GH * GW
    angle = turns_of(ids, stride).astype(np.float64) * (2.0 * math.pi / period)
    cosine, sine = np.cos(angle), np.sin(angle)
    forward, backward, kinds = [], [], []
    for j in pairs:
        forward += [cosine[j], -sine[j]]
        backward += [2.0 * cosine[j], -2.0 * sine[j]]
        kinds.append(1)
    for k in range(0, len(selfs), 2):
        a, b = selfs[k], selfs[k + 1]
        forward += [np.round(cosine[a]), np.round(cosine[b])]
        backward += [np.round(cosine[a]), np.round(cosine[b])]
        kinds.append(0)
    forward = np.stack(forward).astype(np.float32)
    backward = np.stack(backward).T.astype(np.float32)
    return forward, backward, np.array(kinds, np.int32)


def polar_complex(values):
    width = values.shape[-1]
    vals = values.astype(jnp.float32)
    mean_square = jnp.sum(vals * vals) / (2 * width * width)
    scale = 0.75 / (math.sqrt(8.0 * width) * jnp.sqrt(mean_square + 1e-06))
    scaled = (vals * scale).astype(jnp.bfloat16)
    real_part, imag_part = scaled[0], scaled[1]
    stacked = jnp.concatenate([real_part, imag_part], axis=0)
    turned = jnp.concatenate([imag_part, -real_part], axis=0)
    gram = jnp.dot(
        stacked.T, jnp.concatenate([stacked, turned], axis=1), preferred_element_type=jnp.float32
    ).astype(jnp.bfloat16)
    gram_real = gram[:, :width]
    gram_imag = gram[:, width:]
    blocked = jnp.concatenate([gram, jnp.concatenate([-gram_imag, gram_real], axis=1)], axis=0)
    side = jnp.concatenate([real_part, imag_part], axis=1)
    product = jnp.dot(side, blocked, preferred_element_type=jnp.float32)
    result = (1.5 * side.astype(jnp.float32) - 0.5 * product).astype(jnp.bfloat16)
    return jnp.stack([result[:, :width], result[:, width:]], axis=0)


def polar_real(values):
    width = values.shape[-1]
    vals = values.astype(jnp.float32)
    mean_square = jnp.sum(vals * vals, axis=(1, 2), keepdims=True) / (2 * width * width)
    scale = 0.75 / (math.sqrt(8.0 * width) * jnp.sqrt(mean_square + 1e-06))
    scaled = (vals * scale).astype(jnp.bfloat16)
    gram = jnp.einsum("nri,nrj->nij", scaled, scaled, preferred_element_type=jnp.float32).astype(
        jnp.bfloat16
    )
    product = jnp.einsum("nij,njk->nik", scaled, gram, preferred_element_type=jnp.float32)
    return (1.5 * scaled.astype(jnp.float32) - 0.5 * product).astype(jnp.bfloat16)


def on_device(grad_parts, kernel):
    devices_dp = lax.axis_size("dp")
    devices_freq = lax.axis_size("freq")
    devices = devices_dp * devices_freq
    total_freq = KD * devices
    stride = GT * GH * GW // total_freq
    scale_out = math.sqrt(C / total_freq)
    own_width = kernel.shape[1]
    forward, backward, kinds = slot_plan(total_freq, stride)

    gradient = lax.psum_scatter(grad_parts[0], "dp", scatter_dimension=1, tiled=True).reshape(
        TAPS, own_width
    )
    local_square = jnp.sum(gradient * gradient)
    summed = lax.psum(lax.psum(local_square, "freq"), "dp")
    factor = jnp.minimum(1.0, CLIP * math.sqrt(TAPS * C * C) / jnp.sqrt(summed + 1e-06))
    updated = kernel - factor * gradient

    spectra = jnp.dot(jnp.asarray(forward), updated, precision=HIGH).astype(jnp.bfloat16)
    sent = spectra.reshape(devices, 2, own_width)
    whole = lax.all_to_all(sent, AXES, 0, 0, tiled=True)
    matrix = whole.transpose(1, 0, 2).reshape(2, C, C)

    me = lax.axis_index(AXES)
    is_pair = jnp.asarray(kinds)[me] == 1
    polar_part = lax.cond(is_pair, polar_complex, polar_real, matrix)

    back = polar_part.reshape(2, devices, own_width).transpose(1, 0, 2)
    returned = lax.all_to_all(back, AXES, 0, 0, tiled=True)
    planes = returned.reshape(2 * devices, own_width).astype(jnp.float32)
    return jnp.dot(jnp.asarray(backward), planes, precision=HIGH) * scale_out


def solution(mesh):
    return jax.shard_map(
        on_device,
        mesh=mesh,
        in_specs=(P("dp", None, None, "freq"), P(None, ("dp", "freq"))),
        out_specs=P(None, ("dp", "freq")),
        check_vma=False,
    )
```

```python
import math

import numpy as np

import jax
import jax.numpy as jnp
from jax import lax
from jax.sharding import PartitionSpec as P

C = 512
TAPS = 27
GT = 8
GH = 32
GW = 32
KD = 2

CLIP = 0.25
HIGH = lax.Precision.HIGHEST
AXES = ("dp", "freq")


def grid_point(freq_ids, stride):
    flat_index = freq_ids * stride
    return flat_index // (GH * GW), flat_index // GW % GH, flat_index % GW


def turns_of(freq_ids, stride):
    freq_time, freq_row, freq_col = grid_point(freq_ids, stride)
    taps = np.arange(TAPS)
    off_time = taps // 9 - 1
    off_row = taps // 3 % 3 - 1
    off_col = taps % 3 - 1
    period = GT * GH * GW
    return (
        freq_time[:, None] * off_time[None, :] * (GH * GW)
        + freq_row[:, None] * off_row[None, :] * (GT * GW)
        + freq_col[:, None] * off_col[None, :] * (GT * GH)
    ) % period


def tap_phases(freq_ids, stride):
    flat_index = freq_ids * stride
    freq_time = flat_index // (GH * GW)
    freq_row = flat_index // GW % GH
    freq_col = flat_index % GW
    taps = jnp.arange(TAPS, dtype=jnp.int32)
    off_time = taps // 9 - 1
    off_row = taps // 3 % 3 - 1
    off_col = taps % 3 - 1
    period = GT * GH * GW
    turns = (
        freq_time[:, None] * off_time[None, :] * (GH * GW)
        + freq_row[:, None] * off_row[None, :] * (GT * GW)
        + freq_col[:, None] * off_col[None, :] * (GT * GH)
    ) % period
    angle = turns.astype(jnp.float32) * (2.0 * math.pi / period)
    return (jnp.cos(angle), jnp.sin(angle))


def slot_plan(total_freq, stride):
    ids = np.arange(total_freq)
    freq_time, freq_row, freq_col = grid_point(ids, stride)
    key = {(int(a), int(b), int(c)): j for j, (a, b, c) in enumerate(zip(freq_time, freq_row, freq_col))}
    pairs, selfs, seen = [], [], set()
    for j in range(total_freq):
        if j in seen:
            continue
        mate = key[(int(-freq_time[j] % GT), int(-freq_row[j] % GH), int(-freq_col[j] % GW))]
        seen.update((j, mate))
        if mate == j:
            selfs.append(j)
        else:
            pairs.append(j)
    assert len(selfs) % 2 == 0
    period = GT * GH * GW
    angle = turns_of(ids, stride).astype(np.float64) * (2.0 * math.pi / period)
    cosine, sine = np.cos(angle), np.sin(angle)
    forward, backward, kinds = [], [], []
    for j in pairs:
        forward += [(j, 0), (j, 1)]
        backward += [2.0 * cosine[j], -2.0 * sine[j]]
        kinds.append(1)
    for k in range(0, len(selfs), 2):
        a, b = selfs[k], selfs[k + 1]
        forward += [(a, 0), (b, 0)]
        backward += [np.round(cosine[a]), np.round(cosine[b])]
        kinds.append(0)
    forward = np.array(forward, np.int32)
    backward = np.stack(backward).T.astype(np.float32)
    return forward, backward, np.array(kinds, np.int32)


def polar_complex(values):
    width = values.shape[-1]
    vals = values.astype(jnp.float32)
    mean_square = jnp.sum(vals * vals) / (2 * width * width)
    scale = 0.75 / (math.sqrt(8.0 * width) * jnp.sqrt(mean_square + 1e-06))
    scaled = (vals * scale).astype(jnp.bfloat16)
    real_part, imag_part = scaled[0], scaled[1]
    stacked = jnp.concatenate([real_part, imag_part], axis=0)
    turned = jnp.concatenate([imag_part, -real_part], axis=0)
    gram = jnp.dot(
        stacked.T, jnp.concatenate([stacked, turned], axis=1), preferred_element_type=jnp.float32
    ).astype(jnp.bfloat16)
    gram_real = gram[:, :width]
    gram_imag = gram[:, width:]
    blocked = jnp.concatenate([gram, jnp.concatenate([-gram_imag, gram_real], axis=1)], axis=0)
    side = jnp.concatenate([real_part, imag_part], axis=1)
    product = jnp.dot(side, blocked, preferred_element_type=jnp.float32)
    result = (1.5 * side.astype(jnp.float32) - 0.5 * product).astype(jnp.bfloat16)
    return jnp.stack([result[:, :width], result[:, width:]], axis=0)


def polar_real(values):
    width = values.shape[-1]
    vals = values.astype(jnp.float32)
    mean_square = jnp.sum(vals * vals, axis=(1, 2), keepdims=True) / (2 * width * width)
    scale = 0.75 / (math.sqrt(8.0 * width) * jnp.sqrt(mean_square + 1e-06))
    scaled = (vals * scale).astype(jnp.bfloat16)
    gram = jnp.einsum("nri,nrj->nij", scaled, scaled, preferred_element_type=jnp.float32).astype(
        jnp.bfloat16
    )
    product = jnp.einsum("nij,njk->nik", scaled, gram, preferred_element_type=jnp.float32)
    return (1.5 * scaled.astype(jnp.float32) - 0.5 * product).astype(jnp.bfloat16)


def reduce_over_dp(grad_parts, own_width):
    devices_dp = lax.axis_size("dp")
    if devices_dp % 2:
        return lax.psum_scatter(grad_parts[0], "dp", scatter_dimension=1, tiled=True).reshape(
            TAPS, own_width
        )
    d = lax.axis_index("dp")
    core = d % 2
    chips = devices_dp // 2
    parts = grad_parts[0].reshape(TAPS, chips, 2, own_width)
    send = lax.dynamic_index_in_dim(parts, 1 - core, axis=2, keepdims=False)
    keep = lax.dynamic_index_in_dim(parts, core, axis=2, keepdims=False)
    pair = [(i, i ^ 1) for i in range(devices_dp)]
    halves = keep + lax.ppermute(send, "dp", pair)
    if chips == 1:
        return halves.reshape(TAPS, own_width)
    chip = d // 2
    blocks = halves
    width = chips
    level = 1
    while width > 1:
        width //= 2
        bit = (chip // width) % 2
        split = blocks.reshape(TAPS, 2, width, own_width)
        mine = lax.dynamic_index_in_dim(split, bit, axis=1, keepdims=False)
        other = lax.dynamic_index_in_dim(split, 1 - bit, axis=1, keepdims=False)
        stride = 2 * width
        partner = [(i, i ^ stride) for i in range(devices_dp)]
        blocks = mine + lax.ppermute(other, "dp", partner)
        level += 1
    return blocks.reshape(TAPS, own_width)


def total_over_devices(value, devices):
    spread = jnp.broadcast_to(value, (devices, 1))
    gathered = lax.all_to_all(spread, AXES, 0, 0, tiled=True)
    return jnp.sum(gathered)


def on_device(grad_parts, kernel):
    devices_dp = lax.axis_size("dp")
    devices_freq = lax.axis_size("freq")
    devices = devices_dp * devices_freq
    total_freq = KD * devices
    stride = GT * GH * GW // total_freq
    scale_out = math.sqrt(C / total_freq)
    own_width = kernel.shape[1]
    rows, backward, kinds = slot_plan(total_freq, stride)

    gradient = reduce_over_dp(grad_parts, own_width)
    local_square = jnp.sum(gradient * gradient)
    summed = total_over_devices(local_square, devices)
    factor = jnp.minimum(1.0, CLIP * math.sqrt(TAPS * C * C) / jnp.sqrt(summed + 1e-06))
    updated = kernel - factor * gradient

    cosine, sine = tap_phases(jnp.asarray(rows[:, 0]), stride)
    forward = jnp.where(jnp.asarray(rows[:, 1] == 0)[:, None], cosine, -sine)
    spectra = jnp.dot(forward, updated, precision=HIGH).astype(jnp.bfloat16)
    sent = spectra.reshape(devices, 2, own_width)
    whole = lax.all_to_all(sent, AXES, 0, 0, tiled=True)
    matrix = whole.transpose(1, 0, 2).reshape(2, C, C)

    me = lax.axis_index(AXES)
    is_pair = jnp.asarray(kinds)[me] == 1
    polar_part = lax.cond(is_pair, polar_complex, polar_real, matrix)

    back = polar_part.reshape(2, devices, own_width).transpose(1, 0, 2)
    returned = lax.all_to_all(back, AXES, 0, 0, tiled=True)
    planes = returned.reshape(2 * devices, own_width).astype(jnp.float32)
    return jnp.dot(jnp.asarray(backward), planes, precision=HIGH) * scale_out


def solution(mesh):
    return jax.shard_map(
        on_device,
        mesh=mesh,
        in_specs=(P("dp", None, None, "freq"), P(None, ("dp", "freq"))),
        out_specs=P(None, ("dp", "freq")),
        check_vma=False,
    )
```

```python
import math

import numpy as np

import jax
import jax.numpy as jnp
from jax import lax
from jax.sharding import PartitionSpec as P

C = 512
TAPS = 27
GT = 8
GH = 32
GW = 32
KD = 2

CLIP = 0.25
HIGH = lax.Precision.HIGHEST
AXES = ("dp", "freq")


def grid_point(freq_ids, stride):
    flat_index = freq_ids * stride
    return flat_index // (GH * GW), flat_index // GW % GH, flat_index % GW


def turns_of(freq_ids, stride):
    freq_time, freq_row, freq_col = grid_point(freq_ids, stride)
    taps = np.arange(TAPS)
    off_time = taps // 9 - 1
    off_row = taps // 3 % 3 - 1
    off_col = taps % 3 - 1
    period = GT * GH * GW
    return (
        freq_time[:, None] * off_time[None, :] * (GH * GW)
        + freq_row[:, None] * off_row[None, :] * (GT * GW)
        + freq_col[:, None] * off_col[None, :] * (GT * GH)
    ) % period


def tap_phases(freq_ids, stride):
    flat_index = freq_ids * stride
    freq_time = flat_index // (GH * GW)
    freq_row = flat_index // GW % GH
    freq_col = flat_index % GW
    taps = jnp.arange(TAPS, dtype=jnp.int32)
    off_time = taps // 9 - 1
    off_row = taps // 3 % 3 - 1
    off_col = taps % 3 - 1
    period = GT * GH * GW
    turns = (
        freq_time[:, None] * off_time[None, :] * (GH * GW)
        + freq_row[:, None] * off_row[None, :] * (GT * GW)
        + freq_col[:, None] * off_col[None, :] * (GT * GH)
    ) % period
    angle = turns.astype(jnp.float32) * (2.0 * math.pi / period)
    return (jnp.cos(angle), jnp.sin(angle))


def slot_plan(total_freq, stride):
    ids = np.arange(total_freq)
    freq_time, freq_row, freq_col = grid_point(ids, stride)
    key = {(int(a), int(b), int(c)): j for j, (a, b, c) in enumerate(zip(freq_time, freq_row, freq_col))}
    pairs, selfs, seen = [], [], set()
    for j in range(total_freq):
        if j in seen:
            continue
        mate = key[(int(-freq_time[j] % GT), int(-freq_row[j] % GH), int(-freq_col[j] % GW))]
        seen.update((j, mate))
        if mate == j:
            selfs.append(j)
        else:
            pairs.append(j)
    assert len(selfs) % 2 == 0
    period = GT * GH * GW
    angle = turns_of(ids, stride).astype(np.float64) * (2.0 * math.pi / period)
    cosine, sine = np.cos(angle), np.sin(angle)
    forward, backward, kinds = [], [], []
    for j in pairs:
        forward += [(j, 0), (j, 1)]
        backward += [2.0 * cosine[j], -2.0 * sine[j]]
        kinds.append(1)
    for k in range(0, len(selfs), 2):
        a, b = selfs[k], selfs[k + 1]
        forward += [(a, 0), (b, 0)]
        backward += [np.round(cosine[a]), np.round(cosine[b])]
        kinds.append(0)
    forward = np.array(forward, np.int32)
    backward = np.stack(backward).T.astype(np.float32)
    return forward, backward, np.array(kinds, np.int32)


def polar_complex(values):
    width = values.shape[-1]
    vals = values.astype(jnp.float32)
    mean_square = jnp.sum(vals * vals) / (2 * width * width)
    scale = 0.75 / (math.sqrt(8.0 * width) * jnp.sqrt(mean_square + 1e-06))
    scaled = (vals * scale).astype(jnp.bfloat16)
    real_part, imag_part = scaled[0], scaled[1]
    stacked = jnp.concatenate([real_part, imag_part], axis=0)
    turned = jnp.concatenate([imag_part, -real_part], axis=0)
    gram = jnp.dot(
        stacked.T, jnp.concatenate([stacked, turned], axis=1), preferred_element_type=jnp.float32
    ).astype(jnp.bfloat16)
    gram_real = gram[:, :width]
    gram_imag = gram[:, width:]
    blocked = jnp.concatenate([gram, jnp.concatenate([-gram_imag, gram_real], axis=1)], axis=0)
    side = jnp.concatenate([real_part, imag_part], axis=1)
    product = jnp.dot(side, blocked, preferred_element_type=jnp.float32)
    result = (1.5 * side.astype(jnp.float32) - 0.5 * product).astype(jnp.bfloat16)
    return jnp.stack([result[:, :width], result[:, width:]], axis=0)


def polar_real(values):
    width = values.shape[-1]
    vals = values.astype(jnp.float32)
    mean_square = jnp.sum(vals * vals, axis=(1, 2), keepdims=True) / (2 * width * width)
    scale = 0.75 / (math.sqrt(8.0 * width) * jnp.sqrt(mean_square + 1e-06))
    scaled = (vals * scale).astype(jnp.bfloat16)
    gram = jnp.einsum("nri,nrj->nij", scaled, scaled, preferred_element_type=jnp.float32).astype(
        jnp.bfloat16
    )
    product = jnp.einsum("nij,njk->nik", scaled, gram, preferred_element_type=jnp.float32)
    return (1.5 * scaled.astype(jnp.float32) - 0.5 * product).astype(jnp.bfloat16)


def reduce_over_dp(grad_parts, own_width, pieces=2):
    devices_dp = lax.axis_size("dp")
    if devices_dp % 2 or own_width % (128 * pieces):
        return lax.psum_scatter(grad_parts[0], "dp", scatter_dimension=1, tiled=True).reshape(
            TAPS, own_width
        )
    d = lax.axis_index("dp")
    core = d % 2
    chip = d // 2
    chips = devices_dp // 2
    parts = grad_parts[0]
    piece = own_width // pieces
    pair = [(i, i ^ 1) for i in range(devices_dp)]
    outs = []
    for p in range(pieces):
        cols = parts[:, :, p * piece:(p + 1) * piece]

        def gather(c):
            return jnp.stack(
                [lax.dynamic_index_in_dim(cols, 2 * k + c, axis=1, keepdims=False) for k in range(chips)]
            )

        blocks = gather(core) + lax.ppermute(gather(1 - core), "dp", pair)
        width = chips
        while width > 1:
            width //= 2
            bit = (chip // width) % 2
            split = blocks.reshape(2, width, TAPS, piece)
            mine = lax.dynamic_index_in_dim(split, bit, axis=0, keepdims=False)
            other = lax.dynamic_index_in_dim(split, 1 - bit, axis=0, keepdims=False)
            partner = [(i, i ^ (2 * width)) for i in range(devices_dp)]
            blocks = mine + lax.ppermute(other, "dp", partner)
        outs.append(blocks.reshape(TAPS, piece))
    return jnp.concatenate(outs, axis=1)


def total_over_devices(value, devices):
    spread = jnp.broadcast_to(value, (devices, 1))
    gathered = lax.all_to_all(spread, AXES, 0, 0, tiled=True)
    return jnp.sum(gathered)


def on_device(grad_parts, kernel):
    devices_dp = lax.axis_size("dp")
    devices_freq = lax.axis_size("freq")
    devices = devices_dp * devices_freq
    total_freq = KD * devices
    stride = GT * GH * GW // total_freq
    scale_out = math.sqrt(C / total_freq)
    own_width = kernel.shape[1]
    rows, backward, kinds = slot_plan(total_freq, stride)

    gradient = reduce_over_dp(grad_parts, own_width)
    local_square = jnp.sum(gradient * gradient)
    summed = total_over_devices(local_square, devices)
    factor = jnp.minimum(1.0, CLIP * math.sqrt(TAPS * C * C) / jnp.sqrt(summed + 1e-06))
    updated = kernel - factor * gradient

    cosine, sine = tap_phases(jnp.asarray(rows[:, 0]), stride)
    forward = jnp.where(jnp.asarray(rows[:, 1] == 0)[:, None], cosine, -sine)
    spectra = jnp.dot(forward, updated, precision=HIGH).astype(jnp.bfloat16)
    sent = spectra.reshape(devices, 2, own_width)
    whole = lax.all_to_all(sent, AXES, 0, 0, tiled=True)
    matrix = whole.transpose(1, 0, 2).reshape(2, C, C)

    me = lax.axis_index(AXES)
    is_pair = jnp.asarray(kinds)[me] == 1
    polar_part = lax.cond(is_pair, polar_complex, polar_real, matrix)

    back = polar_part.reshape(2, devices, own_width).transpose(1, 0, 2)
    returned = lax.all_to_all(back, AXES, 0, 0, tiled=True)
    planes = returned.reshape(2 * devices, own_width).astype(jnp.float32)
    return jnp.dot(jnp.asarray(backward), planes, precision=HIGH) * scale_out


def solution(mesh):
    return jax.shard_map(
        on_device,
        mesh=mesh,
        in_specs=(P("dp", None, None, "freq"), P(None, ("dp", "freq"))),
        out_specs=P(None, ("dp", "freq")),
        check_vma=False,
    )
```

```python
import math

import numpy as np

import jax
import jax.numpy as jnp
from jax import lax
from jax.sharding import PartitionSpec as P

C = 512
TAPS = 27
GT = 8
GH = 32
GW = 32
KD = 2

CLIP = 0.25
HIGH = lax.Precision.HIGHEST
AXES = ("dp", "freq")


def grid_point(freq_ids, stride):
    flat_index = freq_ids * stride
    return flat_index // (GH * GW), flat_index // GW % GH, flat_index % GW


def turns_of(freq_ids, stride):
    freq_time, freq_row, freq_col = grid_point(freq_ids, stride)
    taps = np.arange(TAPS)
    off_time = taps // 9 - 1
    off_row = taps // 3 % 3 - 1
    off_col = taps % 3 - 1
    period = GT * GH * GW
    return (
        freq_time[:, None] * off_time[None, :] * (GH * GW)
        + freq_row[:, None] * off_row[None, :] * (GT * GW)
        + freq_col[:, None] * off_col[None, :] * (GT * GH)
    ) % period


def tap_phases(freq_ids, stride):
    flat_index = freq_ids * stride
    freq_time = flat_index // (GH * GW)
    freq_row = flat_index // GW % GH
    freq_col = flat_index % GW
    taps = jnp.arange(TAPS, dtype=jnp.int32)
    off_time = taps // 9 - 1
    off_row = taps // 3 % 3 - 1
    off_col = taps % 3 - 1
    period = GT * GH * GW
    turns = (
        freq_time[:, None] * off_time[None, :] * (GH * GW)
        + freq_row[:, None] * off_row[None, :] * (GT * GW)
        + freq_col[:, None] * off_col[None, :] * (GT * GH)
    ) % period
    angle = turns.astype(jnp.float32) * (2.0 * math.pi / period)
    return (jnp.cos(angle), jnp.sin(angle))


def slot_plan(total_freq, stride):
    ids = np.arange(total_freq)
    freq_time, freq_row, freq_col = grid_point(ids, stride)
    key = {(int(a), int(b), int(c)): j for j, (a, b, c) in enumerate(zip(freq_time, freq_row, freq_col))}
    pairs, selfs, seen = [], [], set()
    for j in range(total_freq):
        if j in seen:
            continue
        mate = key[(int(-freq_time[j] % GT), int(-freq_row[j] % GH), int(-freq_col[j] % GW))]
        seen.update((j, mate))
        if mate == j:
            selfs.append(j)
        else:
            pairs.append(j)
    assert len(selfs) % 2 == 0
    period = GT * GH * GW
    angle = turns_of(ids, stride).astype(np.float64) * (2.0 * math.pi / period)
    cosine, sine = np.cos(angle), np.sin(angle)
    forward, backward, kinds = [], [], []
    for j in pairs:
        forward += [(j, 0), (j, 1)]
        backward += [2.0 * cosine[j], -2.0 * sine[j]]
        kinds.append(1)
    for k in range(0, len(selfs), 2):
        a, b = selfs[k], selfs[k + 1]
        forward += [(a, 0), (b, 0)]
        backward += [np.round(cosine[a]), np.round(cosine[b])]
        kinds.append(0)
    forward = np.array(forward, np.int32)
    backward = np.stack(backward).T.astype(np.float32)
    return forward, backward, np.array(kinds, np.int32)


def polar_complex(values):
    width = values.shape[-1]
    vals = values.astype(jnp.float32)
    mean_square = jnp.sum(vals * vals) / (2 * width * width)
    scale = 0.75 / (math.sqrt(8.0 * width) * jnp.sqrt(mean_square + 1e-06))
    scaled = (vals * scale).astype(jnp.bfloat16)
    real_part, imag_part = scaled[0], scaled[1]
    stacked = jnp.concatenate([real_part, imag_part], axis=0)
    turned = jnp.concatenate([imag_part, -real_part], axis=0)
    gram = jnp.dot(
        stacked.T, jnp.concatenate([stacked, turned], axis=1), preferred_element_type=jnp.float32
    ).astype(jnp.bfloat16)
    gram_real = gram[:, :width]
    gram_imag = gram[:, width:]
    blocked = jnp.concatenate([gram, jnp.concatenate([-gram_imag, gram_real], axis=1)], axis=0)
    side = jnp.concatenate([real_part, imag_part], axis=1)
    product = jnp.dot(side, blocked, preferred_element_type=jnp.float32)
    result = (1.5 * side.astype(jnp.float32) - 0.5 * product).astype(jnp.bfloat16)
    return jnp.stack([result[:, :width], result[:, width:]], axis=0)


def polar_real(values):
    width = values.shape[-1]
    vals = values.astype(jnp.float32)
    mean_square = jnp.sum(vals * vals, axis=(1, 2), keepdims=True) / (2 * width * width)
    scale = 0.75 / (math.sqrt(8.0 * width) * jnp.sqrt(mean_square + 1e-06))
    scaled = (vals * scale).astype(jnp.bfloat16)
    gram = jnp.einsum("nri,nrj->nij", scaled, scaled, preferred_element_type=jnp.float32).astype(
        jnp.bfloat16
    )
    product = jnp.einsum("nij,njk->nik", scaled, gram, preferred_element_type=jnp.float32)
    return (1.5 * scaled.astype(jnp.float32) - 0.5 * product).astype(jnp.bfloat16)


def reduce_over_dp(grad_parts, own_width, pieces=2):
    devices_dp = lax.axis_size("dp")
    if devices_dp % 2 or own_width % (128 * pieces):
        return lax.psum_scatter(grad_parts[0], "dp", scatter_dimension=1, tiled=True).reshape(
            TAPS, own_width
        )
    d = lax.axis_index("dp")
    core = d % 2
    chip = d // 2
    chips = devices_dp // 2
    parts = grad_parts[0]
    piece = own_width // pieces
    pair = [(i, i ^ 1) for i in range(devices_dp)]
    outs = []
    for p in range(pieces):
        cols = parts[:, :, p * piece:(p + 1) * piece]

        def gather(c):
            return jnp.stack(
                [lax.dynamic_index_in_dim(cols, 2 * k + c, axis=1, keepdims=False) for k in range(chips)]
            )

        blocks = gather(core) + lax.ppermute(gather(1 - core), "dp", pair)
        width = chips
        while width > 1:
            width //= 2
            bit = (chip // width) % 2
            split = blocks.reshape(2, width, TAPS, piece)
            mine = lax.dynamic_index_in_dim(split, bit, axis=0, keepdims=False)
            other = lax.dynamic_index_in_dim(split, 1 - bit, axis=0, keepdims=False)
            partner = [(i, i ^ (2 * width)) for i in range(devices_dp)]
            blocks = mine + lax.ppermute(other, "dp", partner)
        outs.append(blocks.reshape(TAPS, piece))
    return jnp.concatenate(outs, axis=1)


def total_over_devices(value, devices):
    spread = jnp.broadcast_to(value, (devices, 1))
    gathered = lax.all_to_all(spread, AXES, 0, 0, tiled=True)
    return jnp.sum(gathered)


def tap_groups(total_freq, stride):
    turns = turns_of(np.arange(total_freq), stride)
    groups = {}
    for t in range(TAPS):
        groups.setdefault(tuple(turns[:, t]), []).append(t)
    return list(groups.values())


def group_sums(field, groups):
    return jnp.stack([sum(field[t] for t in group) for group in groups])


def on_device(grad_parts, kernel):
    devices_dp = lax.axis_size("dp")
    devices_freq = lax.axis_size("freq")
    devices = devices_dp * devices_freq
    total_freq = KD * devices
    stride = GT * GH * GW // total_freq
    scale_out = math.sqrt(C / total_freq)
    own_width = kernel.shape[1]
    rows, backward, kinds = slot_plan(total_freq, stride)
    groups = tap_groups(total_freq, stride)
    half = devices_freq // 2
    fi = lax.axis_index("freq")
    side = fi // half
    across = [(i, i ^ half) for i in range(devices_freq)]

    kernel_sums = group_sums(kernel, groups)
    kernel_far = lax.ppermute(kernel_sums, "freq", across)

    gradient = reduce_over_dp(grad_parts, own_width)
    gradient_sums = group_sums(gradient, groups)
    gradient_far = lax.ppermute(gradient_sums, "freq", across)
    local_square = jnp.sum(gradient * gradient)
    summed = total_over_devices(local_square, devices)
    factor = jnp.minimum(1.0, CLIP * math.sqrt(TAPS * C * C) / jnp.sqrt(summed + 1e-06))

    near = kernel_sums - factor * gradient_sums
    far = kernel_far - factor * gradient_far
    first = side == 0
    fields = jnp.stack([jnp.where(first, near, far), jnp.where(first, far, near)], axis=1)

    cosine, sine = tap_phases(jnp.asarray(rows[:, 0]), stride)
    forward = jnp.where(jnp.asarray(rows[:, 1] == 0)[:, None], cosine, -sine)
    forward = forward[:, np.array([group[0] for group in groups])]
    members = [
        [d * devices_freq + h * half + q for d in range(devices_dp) for q in range(half)] for h in range(2)
    ]
    plane_ids = np.array([[2 * s + r for s in members[h] for r in range(2)] for h in range(2)])
    forward_side = lax.dynamic_index_in_dim(forward[plane_ids], side, axis=0, keepdims=False)
    spectra = jnp.dot(
        forward_side, fields.reshape(len(groups), 2 * own_width), precision=HIGH
    ).astype(jnp.bfloat16)
    sent = spectra.reshape(len(members[0]), 2, 2, own_width)
    got = lax.all_to_all(sent, AXES, 0, 0, tiled=True, axis_index_groups=members)
    matrix = (
        got.reshape(devices_dp, half, 2, 2, own_width).transpose(2, 0, 3, 1, 4).reshape(2, C, C)
    )

    me = lax.axis_index(AXES)
    is_pair = jnp.asarray(kinds)[me] == 1
    polar_part = lax.cond(is_pair, polar_complex, polar_real, matrix)

    back = polar_part.reshape(2, devices, own_width).transpose(1, 0, 2)
    returned = lax.all_to_all(back, AXES, 0, 0, tiled=True)
    planes = returned.reshape(2 * devices, own_width).astype(jnp.float32)
    return jnp.dot(jnp.asarray(backward), planes, precision=HIGH) * scale_out


def solution(mesh):
    return jax.shard_map(
        on_device,
        mesh=mesh,
        in_specs=(P("dp", None, None, "freq"), P(None, ("dp", "freq"))),
        out_specs=P(None, ("dp", "freq")),
        check_vma=False,
    )
```

```python
import math

import numpy as np

import jax
import jax.numpy as jnp
from jax import lax
from jax.sharding import PartitionSpec as P

C = 512
TAPS = 27
GT = 8
GH = 32
GW = 32
KD = 2

CLIP = 0.25
HIGH = lax.Precision.HIGHEST
AXES = ("dp", "freq")


def grid_point(freq_ids, stride):
    flat_index = freq_ids * stride
    return flat_index // (GH * GW), flat_index // GW % GH, flat_index % GW


def turns_of(freq_ids, stride):
    freq_time, freq_row, freq_col = grid_point(freq_ids, stride)
    taps = np.arange(TAPS)
    off_time = taps // 9 - 1
    off_row = taps // 3 % 3 - 1
    off_col = taps % 3 - 1
    period = GT * GH * GW
    return (
        freq_time[:, None] * off_time[None, :] * (GH * GW)
        + freq_row[:, None] * off_row[None, :] * (GT * GW)
        + freq_col[:, None] * off_col[None, :] * (GT * GH)
    ) % period


def tap_phases(freq_ids, stride):
    flat_index = freq_ids * stride
    freq_time = flat_index // (GH * GW)
    freq_row = flat_index // GW % GH
    freq_col = flat_index % GW
    taps = jnp.arange(TAPS, dtype=jnp.int32)
    off_time = taps // 9 - 1
    off_row = taps // 3 % 3 - 1
    off_col = taps % 3 - 1
    period = GT * GH * GW
    turns = (
        freq_time[:, None] * off_time[None, :] * (GH * GW)
        + freq_row[:, None] * off_row[None, :] * (GT * GW)
        + freq_col[:, None] * off_col[None, :] * (GT * GH)
    ) % period
    angle = turns.astype(jnp.float32) * (2.0 * math.pi / period)
    return (jnp.cos(angle), jnp.sin(angle))


def slot_plan(total_freq, stride):
    ids = np.arange(total_freq)
    freq_time, freq_row, freq_col = grid_point(ids, stride)
    key = {(int(a), int(b), int(c)): j for j, (a, b, c) in enumerate(zip(freq_time, freq_row, freq_col))}
    pairs, selfs, seen = [], [], set()
    for j in range(total_freq):
        if j in seen:
            continue
        mate = key[(int(-freq_time[j] % GT), int(-freq_row[j] % GH), int(-freq_col[j] % GW))]
        seen.update((j, mate))
        if mate == j:
            selfs.append(j)
        else:
            pairs.append(j)
    assert len(selfs) % 2 == 0
    period = GT * GH * GW
    angle = turns_of(ids, stride).astype(np.float64) * (2.0 * math.pi / period)
    cosine, sine = np.cos(angle), np.sin(angle)
    forward, backward, kinds = [], [], []
    for j in pairs:
        forward += [(j, 0), (j, 1)]
        backward += [2.0 * cosine[j], -2.0 * sine[j]]
        kinds.append(1)
    for k in range(0, len(selfs), 2):
        a, b = selfs[k], selfs[k + 1]
        forward += [(a, 0), (b, 0)]
        backward += [np.round(cosine[a]), np.round(cosine[b])]
        kinds.append(0)
    forward = np.array(forward, np.int32)
    backward = np.stack(backward).T.astype(np.float32)
    return forward, backward, np.array(kinds, np.int32)


def polar_complex(values):
    width = values.shape[-1]
    vals = values.astype(jnp.float32)
    mean_square = jnp.sum(vals * vals) / (2 * width * width)
    scale = 0.75 / (math.sqrt(8.0 * width) * jnp.sqrt(mean_square + 1e-06))
    scaled = (vals * scale).astype(jnp.bfloat16)
    real_part, imag_part = scaled[0], scaled[1]
    stacked = jnp.concatenate([real_part, imag_part], axis=0)
    turned = jnp.concatenate([imag_part, -real_part], axis=0)
    gram = jnp.dot(
        stacked.T, jnp.concatenate([stacked, turned], axis=1), preferred_element_type=jnp.float32
    ).astype(jnp.bfloat16)
    gram_real = gram[:, :width]
    gram_imag = gram[:, width:]
    blocked = jnp.concatenate([gram, jnp.concatenate([-gram_imag, gram_real], axis=1)], axis=0)
    side = jnp.concatenate([real_part, imag_part], axis=1)
    product = jnp.dot(side, blocked, preferred_element_type=jnp.float32)
    result = (1.5 * side.astype(jnp.float32) - 0.5 * product).astype(jnp.bfloat16)
    return jnp.stack([result[:, :width], result[:, width:]], axis=0)


def polar_real(values):
    width = values.shape[-1]
    vals = values.astype(jnp.float32)
    mean_square = jnp.sum(vals * vals, axis=(1, 2), keepdims=True) / (2 * width * width)
    scale = 0.75 / (math.sqrt(8.0 * width) * jnp.sqrt(mean_square + 1e-06))
    scaled = (vals * scale).astype(jnp.bfloat16)
    gram = jnp.einsum("nri,nrj->nij", scaled, scaled, preferred_element_type=jnp.float32).astype(
        jnp.bfloat16
    )
    product = jnp.einsum("nij,njk->nik", scaled, gram, preferred_element_type=jnp.float32)
    return (1.5 * scaled.astype(jnp.float32) - 0.5 * product).astype(jnp.bfloat16)


def reduce_over_dp(grad_parts, own_width, pieces=2):
    devices_dp = lax.axis_size("dp")
    if devices_dp % 2 or own_width % (128 * pieces):
        return [
            lax.psum_scatter(grad_parts[0], "dp", scatter_dimension=1, tiled=True).reshape(
                TAPS, own_width
            )
        ]
    d = lax.axis_index("dp")
    core = d % 2
    chip = d // 2
    chips = devices_dp // 2
    parts = grad_parts[0]
    piece = own_width // pieces
    pair = [(i, i ^ 1) for i in range(devices_dp)]
    outs = []
    for p in range(pieces):
        cols = parts[:, :, p * piece:(p + 1) * piece]

        def gather(c):
            return jnp.stack(
                [lax.dynamic_index_in_dim(cols, 2 * k + c, axis=1, keepdims=False) for k in range(chips)]
            )

        blocks = gather(core) + lax.ppermute(gather(1 - core), "dp", pair)
        width = chips
        while width > 1:
            width //= 2
            bit = (chip // width) % 2
            split = blocks.reshape(2, width, TAPS, piece)
            mine = lax.dynamic_index_in_dim(split, bit, axis=0, keepdims=False)
            other = lax.dynamic_index_in_dim(split, 1 - bit, axis=0, keepdims=False)
            partner = [(i, i ^ (2 * width)) for i in range(devices_dp)]
            blocks = mine + lax.ppermute(other, "dp", partner)
        outs.append(blocks.reshape(TAPS, piece))
    return outs


def total_over_devices(value, devices):
    spread = jnp.broadcast_to(value, (devices, 1))
    gathered = lax.all_to_all(spread, AXES, 0, 0, tiled=True)
    return jnp.sum(gathered)


def tap_groups(total_freq, stride):
    turns = turns_of(np.arange(total_freq), stride)
    groups = {}
    for t in range(TAPS):
        groups.setdefault(tuple(turns[:, t]), []).append(t)
    return list(groups.values())


def group_sums(field, groups):
    return jnp.stack([sum(field[t] for t in group) for group in groups])


def on_device(grad_parts, kernel):
    devices_dp = lax.axis_size("dp")
    devices_freq = lax.axis_size("freq")
    devices = devices_dp * devices_freq
    total_freq = KD * devices
    stride = GT * GH * GW // total_freq
    scale_out = math.sqrt(C / total_freq)
    own_width = kernel.shape[1]
    rows, backward, kinds = slot_plan(total_freq, stride)
    groups = tap_groups(total_freq, stride)
    half = devices_freq // 2
    fi = lax.axis_index("freq")
    side = fi // half
    pairs = [
        [d * devices_freq + q, d * devices_freq + q + half] for d in range(devices_dp) for q in range(half)
    ]

    def swap(value):
        both = lax.all_to_all(
            jnp.stack([value, value]), AXES, 0, 0, tiled=True, axis_index_groups=pairs
        )
        return lax.dynamic_index_in_dim(both, 1 - side, axis=0, keepdims=False)

    kernel_sums = group_sums(kernel, groups)
    kernel_far = swap(kernel_sums)

    pieces = reduce_over_dp(grad_parts, own_width)
    gradient = jnp.concatenate(pieces, axis=1)
    gradient_sums = jnp.concatenate([group_sums(p, groups) for p in pieces], axis=1)
    across = [(i, i ^ half) for i in range(devices_freq)]
    gradient_far = jnp.concatenate(
        [lax.ppermute(group_sums(p, groups), "freq", across) for p in pieces], axis=1
    )
    local_square = jnp.sum(gradient * gradient)
    summed = total_over_devices(local_square, devices)
    factor = jnp.minimum(1.0, CLIP * math.sqrt(TAPS * C * C) / jnp.sqrt(summed + 1e-06))

    near = kernel_sums - factor * gradient_sums
    far = kernel_far - factor * gradient_far
    first = side == 0
    fields = jnp.stack([jnp.where(first, near, far), jnp.where(first, far, near)], axis=1)

    cosine, sine = tap_phases(jnp.asarray(rows[:, 0]), stride)
    forward = jnp.where(jnp.asarray(rows[:, 1] == 0)[:, None], cosine, -sine)
    forward = forward[:, np.array([group[0] for group in groups])]
    members = [
        [d * devices_freq + h * half + q for d in range(devices_dp) for q in range(half)] for h in range(2)
    ]
    plane_ids = np.array([[2 * s + r for s in members[h] for r in range(2)] for h in range(2)])
    forward_side = lax.dynamic_index_in_dim(forward[plane_ids], side, axis=0, keepdims=False)
    spectra = jnp.dot(
        forward_side, fields.reshape(len(groups), 2 * own_width), precision=HIGH
    ).astype(jnp.bfloat16)
    sent = spectra.reshape(len(members[0]), 2, 2, own_width)
    got = lax.all_to_all(sent, AXES, 0, 0, tiled=True, axis_index_groups=members)
    matrix = (
        got.reshape(devices_dp, half, 2, 2, own_width).transpose(2, 0, 3, 1, 4).reshape(2, C, C)
    )

    me = lax.axis_index(AXES)
    is_pair = jnp.asarray(kinds)[me] == 1
    polar_part = lax.cond(is_pair, polar_complex, polar_real, matrix)

    back = polar_part.reshape(2, devices, own_width).transpose(1, 0, 2)
    returned = lax.all_to_all(back, AXES, 0, 0, tiled=True)
    planes = returned.reshape(2 * devices, own_width).astype(jnp.float32)
    return jnp.dot(jnp.asarray(backward), planes, precision=HIGH) * scale_out


def solution(mesh):
    return jax.shard_map(
        on_device,
        mesh=mesh,
        in_specs=(P("dp", None, None, "freq"), P(None, ("dp", "freq"))),
        out_specs=P(None, ("dp", "freq")),
        check_vma=False,
    )
```

```python
import math

import numpy as np

import jax
import jax.numpy as jnp
from jax import lax
from jax.sharding import PartitionSpec as P

C = 512
TAPS = 27
GT = 8
GH = 32
GW = 32
KD = 2

CLIP = 0.25
HIGH = lax.Precision.HIGHEST
AXES = ("dp", "freq")


def grid_point(freq_ids, stride):
    flat_index = freq_ids * stride
    return flat_index // (GH * GW), flat_index // GW % GH, flat_index % GW


def turns_of(freq_ids, stride):
    freq_time, freq_row, freq_col = grid_point(freq_ids, stride)
    taps = np.arange(TAPS)
    off_time = taps // 9 - 1
    off_row = taps // 3 % 3 - 1
    off_col = taps % 3 - 1
    period = GT * GH * GW
    return (
        freq_time[:, None] * off_time[None, :] * (GH * GW)
        + freq_row[:, None] * off_row[None, :] * (GT * GW)
        + freq_col[:, None] * off_col[None, :] * (GT * GH)
    ) % period


def tap_phases(freq_ids, stride):
    flat_index = freq_ids * stride
    freq_time = flat_index // (GH * GW)
    freq_row = flat_index // GW % GH
    freq_col = flat_index % GW
    taps = jnp.arange(TAPS, dtype=jnp.int32)
    off_time = taps // 9 - 1
    off_row = taps // 3 % 3 - 1
    off_col = taps % 3 - 1
    period = GT * GH * GW
    turns = (
        freq_time[:, None] * off_time[None, :] * (GH * GW)
        + freq_row[:, None] * off_row[None, :] * (GT * GW)
        + freq_col[:, None] * off_col[None, :] * (GT * GH)
    ) % period
    angle = turns.astype(jnp.float32) * (2.0 * math.pi / period)
    return (jnp.cos(angle), jnp.sin(angle))


def slot_plan(total_freq, stride):
    ids = np.arange(total_freq)
    freq_time, freq_row, freq_col = grid_point(ids, stride)
    key = {(int(a), int(b), int(c)): j for j, (a, b, c) in enumerate(zip(freq_time, freq_row, freq_col))}
    pairs, selfs, seen = [], [], set()
    for j in range(total_freq):
        if j in seen:
            continue
        mate = key[(int(-freq_time[j] % GT), int(-freq_row[j] % GH), int(-freq_col[j] % GW))]
        seen.update((j, mate))
        if mate == j:
            selfs.append(j)
        else:
            pairs.append(j)
    assert len(selfs) % 2 == 0
    period = GT * GH * GW
    angle = turns_of(ids, stride).astype(np.float64) * (2.0 * math.pi / period)
    cosine, sine = np.cos(angle), np.sin(angle)
    forward, backward, kinds = [], [], []
    for j in pairs:
        forward += [(j, 0), (j, 1)]
        backward += [2.0 * cosine[j], -2.0 * sine[j]]
        kinds.append(1)
    for k in range(0, len(selfs), 2):
        a, b = selfs[k], selfs[k + 1]
        forward += [(a, 0), (b, 0)]
        backward += [np.round(cosine[a]), np.round(cosine[b])]
        kinds.append(0)
    forward = np.array(forward, np.int32)
    backward = np.stack(backward).T.astype(np.float32)
    return forward, backward, np.array(kinds, np.int32)


def polar_complex(values):
    width = values.shape[-1]
    vals = values.astype(jnp.float32)
    mean_square = jnp.sum(vals * vals) / (2 * width * width)
    scale = 0.75 / (math.sqrt(8.0 * width) * jnp.sqrt(mean_square + 1e-06))
    scaled = (vals * scale).astype(jnp.bfloat16)
    real_part, imag_part = scaled[0], scaled[1]
    stacked = jnp.concatenate([real_part, imag_part], axis=0)
    turned = jnp.concatenate([imag_part, -real_part], axis=0)
    gram = jnp.dot(
        stacked.T, jnp.concatenate([stacked, turned], axis=1), preferred_element_type=jnp.float32
    ).astype(jnp.bfloat16)
    gram_real = gram[:, :width]
    gram_imag = gram[:, width:]
    blocked = jnp.concatenate([gram, jnp.concatenate([-gram_imag, gram_real], axis=1)], axis=0)
    side = jnp.concatenate([real_part, imag_part], axis=1)
    product = jnp.dot(side, blocked, preferred_element_type=jnp.float32)
    result = (1.5 * side.astype(jnp.float32) - 0.5 * product).astype(jnp.bfloat16)
    return jnp.stack([result[:, :width], result[:, width:]], axis=0)


def polar_real(values):
    width = values.shape[-1]
    vals = values.astype(jnp.float32)
    mean_square = jnp.sum(vals * vals, axis=(1, 2), keepdims=True) / (2 * width * width)
    scale = 0.75 / (math.sqrt(8.0 * width) * jnp.sqrt(mean_square + 1e-06))
    scaled = (vals * scale).astype(jnp.bfloat16)
    gram = jnp.einsum("nri,nrj->nij", scaled, scaled, preferred_element_type=jnp.float32).astype(
        jnp.bfloat16
    )
    product = jnp.einsum("nij,njk->nik", scaled, gram, preferred_element_type=jnp.float32)
    return (1.5 * scaled.astype(jnp.float32) - 0.5 * product).astype(jnp.bfloat16)


def reduce_over_dp(grad_parts, own_width, pieces=2):
    devices_dp = lax.axis_size("dp")
    half = own_width // 2
    if devices_dp % 2 or half % (128 * pieces):
        return lax.psum_scatter(grad_parts[0], "dp", scatter_dimension=1, tiled=True).reshape(
            TAPS, own_width
        )
    d = lax.axis_index("dp")
    core = d % 2
    chip = d // 2
    chips = devices_dp // 2
    parts = grad_parts[0]
    piece = half // pieces
    pair = [(i, i ^ 1) for i in range(devices_dp)]
    mine, theirs = [], []
    for p in range(pieces):
        keep = lax.dynamic_slice_in_dim(parts, core * half + p * piece, piece, axis=2)
        send = lax.dynamic_slice_in_dim(parts, (1 - core) * half + p * piece, piece, axis=2)
        blocks = (keep + lax.ppermute(send, "dp", pair)).transpose(1, 0, 2)
        blocks = blocks.reshape(chips, 2, TAPS, piece)
        width = chips
        while width > 1:
            width //= 2
            bit = (chip // width) % 2
            split = blocks.reshape(2, width, 2, TAPS, piece)
            near = lax.dynamic_index_in_dim(split, bit, axis=0, keepdims=False)
            far = lax.dynamic_index_in_dim(split, 1 - bit, axis=0, keepdims=False)
            partner = [(i, i ^ (2 * width)) for i in range(devices_dp)]
            blocks = near + lax.ppermute(far, "dp", partner)
        blocks = blocks.reshape(2, TAPS, piece)
        mine.append(lax.dynamic_index_in_dim(blocks, core, axis=0, keepdims=False))
        theirs.append(
            lax.ppermute(lax.dynamic_index_in_dim(blocks, 1 - core, axis=0, keepdims=False), "dp", pair)
        )
    own = jnp.concatenate(mine, axis=1)
    other = jnp.concatenate(theirs, axis=1)
    return jnp.where(core == 0, jnp.concatenate([own, other], axis=1), jnp.concatenate([other, own], axis=1))


def total_over_devices(value, devices):
    spread = jnp.broadcast_to(value, (devices, 1))
    gathered = lax.all_to_all(spread, AXES, 0, 0, tiled=True)
    return jnp.sum(gathered)


def on_device(grad_parts, kernel):
    devices_dp = lax.axis_size("dp")
    devices_freq = lax.axis_size("freq")
    devices = devices_dp * devices_freq
    total_freq = KD * devices
    stride = GT * GH * GW // total_freq
    scale_out = math.sqrt(C / total_freq)
    own_width = kernel.shape[1]
    rows, backward, kinds = slot_plan(total_freq, stride)

    gradient = reduce_over_dp(grad_parts, own_width)
    local_square = jnp.sum(gradient * gradient)
    summed = total_over_devices(local_square, devices)
    factor = jnp.minimum(1.0, CLIP * math.sqrt(TAPS * C * C) / jnp.sqrt(summed + 1e-06))
    updated = kernel - factor * gradient

    cosine, sine = tap_phases(jnp.asarray(rows[:, 0]), stride)
    forward = jnp.where(jnp.asarray(rows[:, 1] == 0)[:, None], cosine, -sine)
    spectra = jnp.dot(forward, updated, precision=HIGH).astype(jnp.bfloat16)
    sent = spectra.reshape(devices, 2, own_width)
    whole = lax.all_to_all(sent, AXES, 0, 0, tiled=True)
    matrix = whole.transpose(1, 0, 2).reshape(2, C, C)

    me = lax.axis_index(AXES)
    is_pair = jnp.asarray(kinds)[me] == 1
    polar_part = lax.cond(is_pair, polar_complex, polar_real, matrix)

    back = polar_part.reshape(2, devices, own_width).transpose(1, 0, 2)
    returned = lax.all_to_all(back, AXES, 0, 0, tiled=True)
    planes = returned.reshape(2 * devices, own_width).astype(jnp.float32)
    return jnp.dot(jnp.asarray(backward), planes, precision=HIGH) * scale_out


def solution(mesh):
    return jax.shard_map(
        on_device,
        mesh=mesh,
        in_specs=(P("dp", None, None, "freq"), P(None, ("dp", "freq"))),
        out_specs=P(None, ("dp", "freq")),
        check_vma=False,
    )
```

```python
import math

import numpy as np

import jax
import jax.numpy as jnp
from jax import lax
from jax.sharding import PartitionSpec as P

C = 512
TAPS = 27
GT = 8
GH = 32
GW = 32
KD = 2

CLIP = 0.25
HIGH = lax.Precision.HIGHEST
AXES = ("dp", "freq")


def grid_point(freq_ids, stride):
    flat_index = freq_ids * stride
    return flat_index // (GH * GW), flat_index // GW % GH, flat_index % GW


def turns_of(freq_ids, stride):
    freq_time, freq_row, freq_col = grid_point(freq_ids, stride)
    taps = np.arange(TAPS)
    off_time = taps // 9 - 1
    off_row = taps // 3 % 3 - 1
    off_col = taps % 3 - 1
    period = GT * GH * GW
    return (
        freq_time[:, None] * off_time[None, :] * (GH * GW)
        + freq_row[:, None] * off_row[None, :] * (GT * GW)
        + freq_col[:, None] * off_col[None, :] * (GT * GH)
    ) % period


def tap_phases(freq_ids, stride):
    flat_index = freq_ids * stride
    freq_time = flat_index // (GH * GW)
    freq_row = flat_index // GW % GH
    freq_col = flat_index % GW
    taps = jnp.arange(TAPS, dtype=jnp.int32)
    off_time = taps // 9 - 1
    off_row = taps // 3 % 3 - 1
    off_col = taps % 3 - 1
    period = GT * GH * GW
    turns = (
        freq_time[:, None] * off_time[None, :] * (GH * GW)
        + freq_row[:, None] * off_row[None, :] * (GT * GW)
        + freq_col[:, None] * off_col[None, :] * (GT * GH)
    ) % period
    angle = turns.astype(jnp.float32) * (2.0 * math.pi / period)
    return (jnp.cos(angle), jnp.sin(angle))


def slot_plan(total_freq, stride):
    ids = np.arange(total_freq)
    freq_time, freq_row, freq_col = grid_point(ids, stride)
    key = {(int(a), int(b), int(c)): j for j, (a, b, c) in enumerate(zip(freq_time, freq_row, freq_col))}
    pairs, selfs, seen = [], [], set()
    for j in range(total_freq):
        if j in seen:
            continue
        mate = key[(int(-freq_time[j] % GT), int(-freq_row[j] % GH), int(-freq_col[j] % GW))]
        seen.update((j, mate))
        if mate == j:
            selfs.append(j)
        else:
            pairs.append(j)
    assert len(selfs) % 2 == 0
    period = GT * GH * GW
    angle = turns_of(ids, stride).astype(np.float64) * (2.0 * math.pi / period)
    cosine, sine = np.cos(angle), np.sin(angle)
    forward, backward, kinds = [], [], []
    for j in pairs:
        forward += [(j, 0), (j, 1)]
        backward += [2.0 * cosine[j], -2.0 * sine[j]]
        kinds.append(1)
    for k in range(0, len(selfs), 2):
        a, b = selfs[k], selfs[k + 1]
        forward += [(a, 0), (b, 0)]
        backward += [np.round(cosine[a]), np.round(cosine[b])]
        kinds.append(0)
    forward = np.array(forward, np.int32)
    backward = np.stack(backward).T.astype(np.float32)
    return forward, backward, np.array(kinds, np.int32)


def polar_complex(values):
    width = values.shape[-1]
    vals = values.astype(jnp.float32)
    mean_square = jnp.sum(vals * vals) / (2 * width * width)
    scale = 0.75 / (math.sqrt(8.0 * width) * jnp.sqrt(mean_square + 1e-06))
    scaled = (vals * scale).astype(jnp.bfloat16)
    real_part, imag_part = scaled[0], scaled[1]
    stacked = jnp.concatenate([real_part, imag_part], axis=0)
    turned = jnp.concatenate([imag_part, -real_part], axis=0)
    gram = jnp.dot(
        stacked.T, jnp.concatenate([stacked, turned], axis=1), preferred_element_type=jnp.float32
    ).astype(jnp.bfloat16)
    gram_real = gram[:, :width]
    gram_imag = gram[:, width:]
    blocked = jnp.concatenate([gram, jnp.concatenate([-gram_imag, gram_real], axis=1)], axis=0)
    side = jnp.concatenate([real_part, imag_part], axis=1)
    product = jnp.dot(side, blocked, preferred_element_type=jnp.float32)
    result = (1.5 * side.astype(jnp.float32) - 0.5 * product).astype(jnp.bfloat16)
    return jnp.stack([result[:, :width], result[:, width:]], axis=0)


def polar_real(values):
    width = values.shape[-1]
    vals = values.astype(jnp.float32)
    mean_square = jnp.sum(vals * vals, axis=(1, 2), keepdims=True) / (2 * width * width)
    scale = 0.75 / (math.sqrt(8.0 * width) * jnp.sqrt(mean_square + 1e-06))
    scaled = (vals * scale).astype(jnp.bfloat16)
    gram = jnp.einsum("nri,nrj->nij", scaled, scaled, preferred_element_type=jnp.float32).astype(
        jnp.bfloat16
    )
    product = jnp.einsum("nij,njk->nik", scaled, gram, preferred_element_type=jnp.float32)
    return (1.5 * scaled.astype(jnp.float32) - 0.5 * product).astype(jnp.bfloat16)


def piece_widths(width):
    tiles = width // 128
    first = max(1, (tiles * 3) // 8)
    return [first * 128, width - first * 128] if tiles > 1 else [width]


def reduce_over_dp(grad_parts, own_width):
    devices_dp = lax.axis_size("dp")
    half = own_width // 2
    if devices_dp % 2 or half % 128:
        return lax.psum_scatter(grad_parts[0], "dp", scatter_dimension=1, tiled=True).reshape(
            TAPS, own_width
        )
    d = lax.axis_index("dp")
    core = d % 2
    chip = d // 2
    chips = devices_dp // 2
    parts = grad_parts[0]
    pair = [(i, i ^ 1) for i in range(devices_dp)]
    mine, theirs = [], []
    offset = 0
    for piece in piece_widths(half):
        keep = lax.dynamic_slice_in_dim(parts, core * half + offset, piece, axis=2)
        send = lax.dynamic_slice_in_dim(parts, (1 - core) * half + offset, piece, axis=2)
        offset += piece
        blocks = (keep + lax.ppermute(send, "dp", pair)).transpose(1, 0, 2)
        blocks = blocks.reshape(chips, 2, TAPS, piece)
        width = chips
        while width > 1:
            width //= 2
            bit = (chip // width) % 2
            split = blocks.reshape(2, width, 2, TAPS, piece)
            near = lax.dynamic_index_in_dim(split, bit, axis=0, keepdims=False)
            far = lax.dynamic_index_in_dim(split, 1 - bit, axis=0, keepdims=False)
            partner = [(i, i ^ (2 * width)) for i in range(devices_dp)]
            blocks = near + lax.ppermute(far, "dp", partner)
        blocks = blocks.reshape(2, TAPS, piece)
        mine.append(lax.dynamic_index_in_dim(blocks, core, axis=0, keepdims=False))
        theirs.append(
            lax.ppermute(lax.dynamic_index_in_dim(blocks, 1 - core, axis=0, keepdims=False), "dp", pair)
        )
    own = jnp.concatenate(mine, axis=1)
    other = jnp.concatenate(theirs, axis=1)
    return jnp.where(core == 0, jnp.concatenate([own, other], axis=1), jnp.concatenate([other, own], axis=1))


def total_over_devices(value, devices):
    spread = jnp.broadcast_to(value, (devices, 1))
    gathered = lax.all_to_all(spread, AXES, 0, 0, tiled=True)
    return jnp.sum(gathered)


def on_device(grad_parts, kernel):
    devices_dp = lax.axis_size("dp")
    devices_freq = lax.axis_size("freq")
    devices = devices_dp * devices_freq
    total_freq = KD * devices
    stride = GT * GH * GW // total_freq
    scale_out = math.sqrt(C / total_freq)
    own_width = kernel.shape[1]
    rows, backward, kinds = slot_plan(total_freq, stride)

    gradient = reduce_over_dp(grad_parts, own_width)
    local_square = jnp.sum(gradient * gradient)
    summed = total_over_devices(local_square, devices)
    factor = jnp.minimum(1.0, CLIP * math.sqrt(TAPS * C * C) / jnp.sqrt(summed + 1e-06))
    updated = kernel - factor * gradient

    cosine, sine = tap_phases(jnp.asarray(rows[:, 0]), stride)
    forward = jnp.where(jnp.asarray(rows[:, 1] == 0)[:, None], cosine, -sine)
    spectra = jnp.dot(forward, updated, precision=HIGH).astype(jnp.bfloat16)
    sent = spectra.reshape(devices, 2, own_width)
    whole = lax.all_to_all(sent, AXES, 0, 0, tiled=True)
    matrix = whole.transpose(1, 0, 2).reshape(2, C, C)

    me = lax.axis_index(AXES)
    is_pair = jnp.asarray(kinds)[me] == 1
    polar_part = lax.cond(is_pair, polar_complex, polar_real, matrix)

    back = polar_part.reshape(2, devices, own_width).transpose(1, 0, 2)
    returned = lax.all_to_all(back, AXES, 0, 0, tiled=True)
    planes = returned.reshape(2 * devices, own_width).astype(jnp.float32)
    return jnp.dot(jnp.asarray(backward), planes, precision=HIGH) * scale_out


def solution(mesh):
    return jax.shard_map(
        on_device,
        mesh=mesh,
        in_specs=(P("dp", None, None, "freq"), P(None, ("dp", "freq"))),
        out_specs=P(None, ("dp", "freq")),
        check_vma=False,
    )
```

```python
import math

import numpy as np

import jax
import jax.numpy as jnp
from jax import lax
from jax.sharding import PartitionSpec as P

C = 512
TAPS = 27
GT = 8
GH = 32
GW = 32
KD = 2

CLIP = 0.25
HIGH = lax.Precision.HIGHEST
AXES = ("dp", "freq")


def grid_point(freq_ids, stride):
    flat_index = freq_ids * stride
    return flat_index // (GH * GW), flat_index // GW % GH, flat_index % GW


def turns_of(freq_ids, stride):
    freq_time, freq_row, freq_col = grid_point(freq_ids, stride)
    taps = np.arange(TAPS)
    off_time = taps // 9 - 1
    off_row = taps // 3 % 3 - 1
    off_col = taps % 3 - 1
    period = GT * GH * GW
    return (
        freq_time[:, None] * off_time[None, :] * (GH * GW)
        + freq_row[:, None] * off_row[None, :] * (GT * GW)
        + freq_col[:, None] * off_col[None, :] * (GT * GH)
    ) % period


def tap_phases(freq_ids, stride):
    flat_index = freq_ids * stride
    freq_time = flat_index // (GH * GW)
    freq_row = flat_index // GW % GH
    freq_col = flat_index % GW
    taps = jnp.arange(TAPS, dtype=jnp.int32)
    off_time = taps // 9 - 1
    off_row = taps // 3 % 3 - 1
    off_col = taps % 3 - 1
    period = GT * GH * GW
    turns = (
        freq_time[:, None] * off_time[None, :] * (GH * GW)
        + freq_row[:, None] * off_row[None, :] * (GT * GW)
        + freq_col[:, None] * off_col[None, :] * (GT * GH)
    ) % period
    angle = turns.astype(jnp.float32) * (2.0 * math.pi / period)
    return (jnp.cos(angle), jnp.sin(angle))


def slot_plan(total_freq, stride):
    ids = np.arange(total_freq)
    freq_time, freq_row, freq_col = grid_point(ids, stride)
    key = {(int(a), int(b), int(c)): j for j, (a, b, c) in enumerate(zip(freq_time, freq_row, freq_col))}
    pairs, selfs, seen = [], [], set()
    for j in range(total_freq):
        if j in seen:
            continue
        mate = key[(int(-freq_time[j] % GT), int(-freq_row[j] % GH), int(-freq_col[j] % GW))]
        seen.update((j, mate))
        if mate == j:
            selfs.append(j)
        else:
            pairs.append(j)
    assert len(selfs) % 2 == 0
    period = GT * GH * GW
    angle = turns_of(ids, stride).astype(np.float64) * (2.0 * math.pi / period)
    cosine, sine = np.cos(angle), np.sin(angle)
    forward, backward, kinds = [], [], []
    for j in pairs:
        forward += [(j, 0), (j, 1)]
        backward += [2.0 * cosine[j], -2.0 * sine[j]]
        kinds.append(1)
    for k in range(0, len(selfs), 2):
        a, b = selfs[k], selfs[k + 1]
        forward += [(a, 0), (b, 0)]
        backward += [np.round(cosine[a]), np.round(cosine[b])]
        kinds.append(0)
    forward = np.array(forward, np.int32)
    backward = np.stack(backward).T.astype(np.float32)
    return forward, backward, np.array(kinds, np.int32)


def polar_complex(values):
    width = values.shape[-1]
    vals = values.astype(jnp.float32)
    mean_square = jnp.sum(vals * vals) / (2 * width * width)
    scale = 0.75 / (math.sqrt(8.0 * width) * jnp.sqrt(mean_square + 1e-06))
    scaled = (vals * scale).astype(jnp.bfloat16)
    real_part, imag_part = scaled[0], scaled[1]
    stacked = jnp.concatenate([real_part, imag_part], axis=0)
    turned = jnp.concatenate([imag_part, -real_part], axis=0)
    gram = jnp.dot(
        stacked.T, jnp.concatenate([stacked, turned], axis=1), preferred_element_type=jnp.float32
    ).astype(jnp.bfloat16)
    gram_real = gram[:, :width]
    gram_imag = gram[:, width:]
    blocked = jnp.concatenate([gram, jnp.concatenate([-gram_imag, gram_real], axis=1)], axis=0)
    side = jnp.concatenate([real_part, imag_part], axis=1)
    product = jnp.dot(side, blocked, preferred_element_type=jnp.float32)
    result = (1.5 * side.astype(jnp.float32) - 0.5 * product).astype(jnp.bfloat16)
    return jnp.stack([result[:, :width], result[:, width:]], axis=0)


def polar_real(values):
    width = values.shape[-1]
    vals = values.astype(jnp.float32)
    mean_square = jnp.sum(vals * vals, axis=(1, 2), keepdims=True) / (2 * width * width)
    scale = 0.75 / (math.sqrt(8.0 * width) * jnp.sqrt(mean_square + 1e-06))
    scaled = (vals * scale).astype(jnp.bfloat16)
    gram = jnp.einsum("nri,nrj->nij", scaled, scaled, preferred_element_type=jnp.float32).astype(
        jnp.bfloat16
    )
    product = jnp.einsum("nij,njk->nik", scaled, gram, preferred_element_type=jnp.float32)
    return (1.5 * scaled.astype(jnp.float32) - 0.5 * product).astype(jnp.bfloat16)


def piece_widths(width):
    tiles = width // 128
    first = max(1, (tiles * 3) // 8)
    return [first * 128, width - first * 128] if tiles > 1 else [width]


def reduce_over_dp(grad_parts, own_width):
    devices_dp = lax.axis_size("dp")
    half = own_width // 2
    if devices_dp % 2 or half % 128:
        gradient = lax.psum_scatter(grad_parts[0], "dp", scatter_dimension=1, tiled=True).reshape(
            TAPS, own_width
        )
        return gradient, jnp.sum(gradient * gradient)
    d = lax.axis_index("dp")
    core = d % 2
    chip = d // 2
    chips = devices_dp // 2
    parts = grad_parts[0]
    pair = [(i, i ^ 1) for i in range(devices_dp)]
    mine, theirs, squares = [], [], []
    offset = 0
    for piece in piece_widths(half):
        keep = lax.dynamic_slice_in_dim(parts, core * half + offset, piece, axis=2)
        send = lax.dynamic_slice_in_dim(parts, (1 - core) * half + offset, piece, axis=2)
        offset += piece
        blocks = (keep + lax.ppermute(send, "dp", pair)).transpose(1, 0, 2)
        blocks = blocks.reshape(chips, 2, TAPS, piece)
        width = chips
        while width > 1:
            width //= 2
            bit = (chip // width) % 2
            split = blocks.reshape(2, width, 2, TAPS, piece)
            near = lax.dynamic_index_in_dim(split, bit, axis=0, keepdims=False)
            far = lax.dynamic_index_in_dim(split, 1 - bit, axis=0, keepdims=False)
            partner = [(i, i ^ (2 * width)) for i in range(devices_dp)]
            blocks = near + lax.ppermute(far, "dp", partner)
        blocks = blocks.reshape(2, TAPS, piece)
        squares.append(jnp.sum(blocks * blocks))
        mine.append(lax.dynamic_index_in_dim(blocks, core, axis=0, keepdims=False))
        theirs.append(
            lax.ppermute(lax.dynamic_index_in_dim(blocks, 1 - core, axis=0, keepdims=False), "dp", pair)
        )
    own = jnp.concatenate(mine, axis=1)
    other = jnp.concatenate(theirs, axis=1)
    gradient = jnp.where(
        core == 0, jnp.concatenate([own, other], axis=1), jnp.concatenate([other, own], axis=1)
    )
    return gradient, sum(squares)


def total_over_devices(value, devices):
    spread = jnp.broadcast_to(value, (devices, 1))
    gathered = lax.all_to_all(spread, AXES, 0, 0, tiled=True)
    return jnp.sum(gathered)


def on_device(grad_parts, kernel):
    devices_dp = lax.axis_size("dp")
    devices_freq = lax.axis_size("freq")
    devices = devices_dp * devices_freq
    total_freq = KD * devices
    stride = GT * GH * GW // total_freq
    scale_out = math.sqrt(C / total_freq)
    own_width = kernel.shape[1]
    rows, backward, kinds = slot_plan(total_freq, stride)

    gradient, local_square = reduce_over_dp(grad_parts, own_width)
    summed = total_over_devices(local_square, devices)
    factor = jnp.minimum(1.0, CLIP * math.sqrt(TAPS * C * C) / jnp.sqrt(summed + 1e-06))
    updated = kernel - factor * gradient

    cosine, sine = tap_phases(jnp.asarray(rows[:, 0]), stride)
    forward = jnp.where(jnp.asarray(rows[:, 1] == 0)[:, None], cosine, -sine)
    spectra = jnp.dot(forward, updated, precision=HIGH).astype(jnp.bfloat16)
    sent = spectra.reshape(devices, 2, own_width)
    whole = lax.all_to_all(sent, AXES, 0, 0, tiled=True)
    matrix = whole.transpose(1, 0, 2).reshape(2, C, C)

    me = lax.axis_index(AXES)
    is_pair = jnp.asarray(kinds)[me] == 1
    polar_part = lax.cond(is_pair, polar_complex, polar_real, matrix)

    back = polar_part.reshape(2, devices, own_width).transpose(1, 0, 2)
    returned = lax.all_to_all(back, AXES, 0, 0, tiled=True)
    planes = returned.reshape(2 * devices, own_width).astype(jnp.float32)
    return jnp.dot(jnp.asarray(backward), planes, precision=HIGH) * scale_out


def solution(mesh):
    return jax.shard_map(
        on_device,
        mesh=mesh,
        in_specs=(P("dp", None, None, "freq"), P(None, ("dp", "freq"))),
        out_specs=P(None, ("dp", "freq")),
        check_vma=False,
    )
```

```python
import math

import numpy as np

import jax
import jax.numpy as jnp
from jax import lax
from jax.sharding import PartitionSpec as P

C = 512
TAPS = 27
GT = 8
GH = 32
GW = 32
KD = 2

CLIP = 0.25
HIGH = lax.Precision.HIGHEST
AXES = ("dp", "freq")


def grid_point(freq_ids, stride):
    flat_index = freq_ids * stride
    return flat_index // (GH * GW), flat_index // GW % GH, flat_index % GW


def turns_of(freq_ids, stride):
    freq_time, freq_row, freq_col = grid_point(freq_ids, stride)
    taps = np.arange(TAPS)
    off_time = taps // 9 - 1
    off_row = taps // 3 % 3 - 1
    off_col = taps % 3 - 1
    period = GT * GH * GW
    return (
        freq_time[:, None] * off_time[None, :] * (GH * GW)
        + freq_row[:, None] * off_row[None, :] * (GT * GW)
        + freq_col[:, None] * off_col[None, :] * (GT * GH)
    ) % period


def tap_phases(freq_ids, stride):
    flat_index = freq_ids * stride
    freq_time = flat_index // (GH * GW)
    freq_row = flat_index // GW % GH
    freq_col = flat_index % GW
    taps = jnp.arange(TAPS, dtype=jnp.int32)
    off_time = taps // 9 - 1
    off_row = taps // 3 % 3 - 1
    off_col = taps % 3 - 1
    period = GT * GH * GW
    turns = (
        freq_time[:, None] * off_time[None, :] * (GH * GW)
        + freq_row[:, None] * off_row[None, :] * (GT * GW)
        + freq_col[:, None] * off_col[None, :] * (GT * GH)
    ) % period
    angle = turns.astype(jnp.float32) * (2.0 * math.pi / period)
    return (jnp.cos(angle), jnp.sin(angle))


def slot_plan(total_freq, stride):
    ids = np.arange(total_freq)
    freq_time, freq_row, freq_col = grid_point(ids, stride)
    key = {(int(a), int(b), int(c)): j for j, (a, b, c) in enumerate(zip(freq_time, freq_row, freq_col))}
    pairs, selfs, seen = [], [], set()
    for j in range(total_freq):
        if j in seen:
            continue
        mate = key[(int(-freq_time[j] % GT), int(-freq_row[j] % GH), int(-freq_col[j] % GW))]
        seen.update((j, mate))
        if mate == j:
            selfs.append(j)
        else:
            pairs.append(j)
    assert len(selfs) % 2 == 0
    period = GT * GH * GW
    angle = turns_of(ids, stride).astype(np.float64) * (2.0 * math.pi / period)
    cosine, sine = np.cos(angle), np.sin(angle)
    forward, backward, kinds = [], [], []
    for j in pairs:
        forward += [(j, 0), (j, 1)]
        backward += [2.0 * cosine[j], -2.0 * sine[j]]
        kinds.append(1)
    for k in range(0, len(selfs), 2):
        a, b = selfs[k], selfs[k + 1]
        forward += [(a, 0), (b, 0)]
        backward += [np.round(cosine[a]), np.round(cosine[b])]
        kinds.append(0)
    forward = np.array(forward, np.int32)
    backward = np.stack(backward).T.astype(np.float32)
    return forward, backward, np.array(kinds, np.int32)


def polar_complex(values):
    width = values.shape[-1]
    vals = values.astype(jnp.float32)
    mean_square = jnp.sum(vals * vals) / (2 * width * width)
    scale = 0.75 / (math.sqrt(8.0 * width) * jnp.sqrt(mean_square + 1e-06))
    scaled = (vals * scale).astype(jnp.bfloat16)
    real_part, imag_part = scaled[0], scaled[1]
    stacked = jnp.concatenate([real_part, imag_part], axis=0)
    turned = jnp.concatenate([imag_part, -real_part], axis=0)
    gram = jnp.dot(
        stacked.T, jnp.concatenate([stacked, turned], axis=1), preferred_element_type=jnp.float32
    ).astype(jnp.bfloat16)
    gram_real = gram[:, :width]
    gram_imag = gram[:, width:]
    blocked = jnp.concatenate([gram, jnp.concatenate([-gram_imag, gram_real], axis=1)], axis=0)
    side = jnp.concatenate([real_part, imag_part], axis=1)
    product = jnp.dot(side, blocked, preferred_element_type=jnp.float32)
    result = (1.5 * side.astype(jnp.float32) - 0.5 * product).astype(jnp.bfloat16)
    return jnp.stack([result[:, :width], result[:, width:]], axis=0)


def polar_real(values):
    width = values.shape[-1]
    vals = values.astype(jnp.float32)
    mean_square = jnp.sum(vals * vals, axis=(1, 2), keepdims=True) / (2 * width * width)
    scale = 0.75 / (math.sqrt(8.0 * width) * jnp.sqrt(mean_square + 1e-06))
    scaled = (vals * scale).astype(jnp.bfloat16)
    gram = jnp.einsum("nri,nrj->nij", scaled, scaled, preferred_element_type=jnp.float32).astype(
        jnp.bfloat16
    )
    product = jnp.einsum("nij,njk->nik", scaled, gram, preferred_element_type=jnp.float32)
    return (1.5 * scaled.astype(jnp.float32) - 0.5 * product).astype(jnp.bfloat16)


def piece_widths(width):
    tiles = width // 128
    first = max(1, (tiles * 3) // 8)
    return [first * 128, width - first * 128] if tiles > 1 else [width]


def tap_groups(total_freq, stride):
    turns = turns_of(np.arange(total_freq), stride)
    groups = {}
    for t in range(TAPS):
        groups.setdefault(tuple(turns[:, t]), []).append(t)
    return list(groups.values())


def group_sums(field, groups, axis=0):
    taps = [lax.index_in_dim(field, t, axis=axis, keepdims=False) for t in range(TAPS)]
    return jnp.stack([sum(taps[t] for t in group) for group in groups], axis=axis)


def reduce_over_dp(grad_parts, own_width, groups):
    devices_dp = lax.axis_size("dp")
    half = own_width // 2
    if devices_dp % 2 or half % 128:
        gradient = lax.psum_scatter(grad_parts[0], "dp", scatter_dimension=1, tiled=True).reshape(
            TAPS, own_width
        )
        return group_sums(gradient, groups), jnp.sum(gradient * gradient)
    d = lax.axis_index("dp")
    core = d % 2
    chip = d // 2
    chips = devices_dp // 2
    narrow = chips == 2 and 2 * len(groups) + TAPS < 2 * TAPS
    parts = grad_parts[0]
    pair = [(i, i ^ 1) for i in range(devices_dp)]
    mine, theirs, squares = [], [], []
    offset = 0
    for piece in piece_widths(half):
        keep = lax.dynamic_slice_in_dim(parts, core * half + offset, piece, axis=2)
        send = lax.dynamic_slice_in_dim(parts, (1 - core) * half + offset, piece, axis=2)
        offset += piece
        blocks = (keep + lax.ppermute(send, "dp", pair)).transpose(1, 0, 2)
        blocks = blocks.reshape(chips, 2, TAPS, piece)
        if narrow:
            near = lax.dynamic_index_in_dim(blocks, chip, axis=0, keepdims=False)
            far = lax.dynamic_index_in_dim(blocks, 1 - chip, axis=0, keepdims=False)
            partner = [(i, i ^ 2) for i in range(devices_dp)]
            far_sums = lax.ppermute(group_sums(far, groups, axis=1), "dp", partner)
            far_taps = lax.ppermute(far.astype(jnp.bfloat16), "dp", partner)
            sums = group_sums(near, groups, axis=1) + far_sums
            whole = near + far_taps.astype(jnp.float32)
            squares.append(jnp.sum(whole * whole))
        else:
            width = chips
            while width > 1:
                width //= 2
                bit = (chip // width) % 2
                split = blocks.reshape(2, width, 2, TAPS, piece)
                near = lax.dynamic_index_in_dim(split, bit, axis=0, keepdims=False)
                far = lax.dynamic_index_in_dim(split, 1 - bit, axis=0, keepdims=False)
                partner = [(i, i ^ (2 * width)) for i in range(devices_dp)]
                blocks = near + lax.ppermute(far, "dp", partner)
            blocks = blocks.reshape(2, TAPS, piece)
            squares.append(jnp.sum(blocks * blocks))
            sums = group_sums(blocks, groups, axis=1)
        mine.append(lax.dynamic_index_in_dim(sums, core, axis=0, keepdims=False))
        theirs.append(
            lax.ppermute(lax.dynamic_index_in_dim(sums, 1 - core, axis=0, keepdims=False), "dp", pair)
        )
    own = jnp.concatenate(mine, axis=1)
    other = jnp.concatenate(theirs, axis=1)
    gradient_sums = jnp.where(
        core == 0, jnp.concatenate([own, other], axis=1), jnp.concatenate([other, own], axis=1)
    )
    return gradient_sums, sum(squares)


def total_over_devices(value, devices):
    spread = jnp.broadcast_to(value, (devices, 1))
    gathered = lax.all_to_all(spread, AXES, 0, 0, tiled=True)
    return jnp.sum(gathered)


def on_device(grad_parts, kernel):
    devices_dp = lax.axis_size("dp")
    devices_freq = lax.axis_size("freq")
    devices = devices_dp * devices_freq
    total_freq = KD * devices
    stride = GT * GH * GW // total_freq
    scale_out = math.sqrt(C / total_freq)
    own_width = kernel.shape[1]
    rows, backward, kinds = slot_plan(total_freq, stride)

    groups = tap_groups(total_freq, stride)
    gradient_sums, local_square = reduce_over_dp(grad_parts, own_width, groups)
    summed = total_over_devices(local_square, devices)
    factor = jnp.minimum(1.0, CLIP * math.sqrt(TAPS * C * C) / jnp.sqrt(summed + 1e-06))
    updated = group_sums(kernel, groups) - factor * gradient_sums

    cosine, sine = tap_phases(jnp.asarray(rows[:, 0]), stride)
    forward = jnp.where(jnp.asarray(rows[:, 1] == 0)[:, None], cosine, -sine)
    forward = forward[:, np.array([group[0] for group in groups])]
    spectra = jnp.dot(forward, updated, precision=HIGH).astype(jnp.bfloat16)
    sent = spectra.reshape(devices, 2, own_width)
    whole = lax.all_to_all(sent, AXES, 0, 0, tiled=True)
    matrix = whole.transpose(1, 0, 2).reshape(2, C, C)

    me = lax.axis_index(AXES)
    is_pair = jnp.asarray(kinds)[me] == 1
    polar_part = lax.cond(is_pair, polar_complex, polar_real, matrix)

    back = polar_part.reshape(2, devices, own_width).transpose(1, 0, 2)
    returned = lax.all_to_all(back, AXES, 0, 0, tiled=True)
    planes = returned.reshape(2 * devices, own_width).astype(jnp.float32)
    return jnp.dot(jnp.asarray(backward), planes, precision=HIGH) * scale_out


def solution(mesh):
    return jax.shard_map(
        on_device,
        mesh=mesh,
        in_specs=(P("dp", None, None, "freq"), P(None, ("dp", "freq"))),
        out_specs=P(None, ("dp", "freq")),
        check_vma=False,
    )
```

```python
import math

import numpy as np

import jax
import jax.numpy as jnp
from jax import lax
from jax.sharding import PartitionSpec as P

C = 512
TAPS = 27
GT = 8
GH = 32
GW = 32
KD = 2

CLIP = 0.25
HIGH = lax.Precision.HIGHEST
AXES = ("dp", "freq")


def grid_point(freq_ids, stride):
    flat_index = freq_ids * stride
    return flat_index // (GH * GW), flat_index // GW % GH, flat_index % GW


def turns_of(freq_ids, stride):
    freq_time, freq_row, freq_col = grid_point(freq_ids, stride)
    taps = np.arange(TAPS)
    off_time = taps // 9 - 1
    off_row = taps // 3 % 3 - 1
    off_col = taps % 3 - 1
    period = GT * GH * GW
    return (
        freq_time[:, None] * off_time[None, :] * (GH * GW)
        + freq_row[:, None] * off_row[None, :] * (GT * GW)
        + freq_col[:, None] * off_col[None, :] * (GT * GH)
    ) % period


def tap_phases(freq_ids, stride):
    flat_index = freq_ids * stride
    freq_time = flat_index // (GH * GW)
    freq_row = flat_index // GW % GH
    freq_col = flat_index % GW
    taps = jnp.arange(TAPS, dtype=jnp.int32)
    off_time = taps // 9 - 1
    off_row = taps // 3 % 3 - 1
    off_col = taps % 3 - 1
    period = GT * GH * GW
    turns = (
        freq_time[:, None] * off_time[None, :] * (GH * GW)
        + freq_row[:, None] * off_row[None, :] * (GT * GW)
        + freq_col[:, None] * off_col[None, :] * (GT * GH)
    ) % period
    angle = turns.astype(jnp.float32) * (2.0 * math.pi / period)
    return (jnp.cos(angle), jnp.sin(angle))


def slot_plan(total_freq, stride):
    ids = np.arange(total_freq)
    freq_time, freq_row, freq_col = grid_point(ids, stride)
    key = {(int(a), int(b), int(c)): j for j, (a, b, c) in enumerate(zip(freq_time, freq_row, freq_col))}
    pairs, selfs, seen = [], [], set()
    for j in range(total_freq):
        if j in seen:
            continue
        mate = key[(int(-freq_time[j] % GT), int(-freq_row[j] % GH), int(-freq_col[j] % GW))]
        seen.update((j, mate))
        if mate == j:
            selfs.append(j)
        else:
            pairs.append(j)
    assert len(selfs) % 2 == 0
    period = GT * GH * GW
    angle = turns_of(ids, stride).astype(np.float64) * (2.0 * math.pi / period)
    cosine, sine = np.cos(angle), np.sin(angle)
    forward, backward, kinds = [], [], []
    for j in pairs:
        forward += [(j, 0), (j, 1)]
        backward += [2.0 * cosine[j], -2.0 * sine[j]]
        kinds.append(1)
    for k in range(0, len(selfs), 2):
        a, b = selfs[k], selfs[k + 1]
        forward += [(a, 0), (b, 0)]
        backward += [np.round(cosine[a]), np.round(cosine[b])]
        kinds.append(0)
    forward = np.array(forward, np.int32)
    backward = np.stack(backward).T.astype(np.float32)
    return forward, backward, np.array(kinds, np.int32)


def to_matrix(blocks):
    return blocks.transpose(1, 0, 2).reshape(2, C, C)


def to_blocks(matrix, sources):
    return matrix.reshape(2, sources, -1).transpose(1, 0, 2)


def polar_complex(blocks):
    values = to_matrix(blocks)
    width = values.shape[-1]
    vals = values.astype(jnp.float32)
    mean_square = jnp.sum(vals * vals) / (2 * width * width)
    scale = 0.75 / (math.sqrt(8.0 * width) * jnp.sqrt(mean_square + 1e-06))
    scaled = (vals * scale).astype(jnp.bfloat16)
    real_part, imag_part = scaled[0], scaled[1]
    stacked = jnp.concatenate([real_part, imag_part], axis=0)
    turned = jnp.concatenate([imag_part, -real_part], axis=0)
    gram = jnp.dot(
        stacked.T, jnp.concatenate([stacked, turned], axis=1), preferred_element_type=jnp.float32
    ).astype(jnp.bfloat16)
    gram_real = gram[:, :width]
    gram_imag = gram[:, width:]
    blocked = jnp.concatenate([gram, jnp.concatenate([-gram_imag, gram_real], axis=1)], axis=0)
    side = jnp.concatenate([real_part, imag_part], axis=1)
    product = jnp.dot(side, blocked, preferred_element_type=jnp.float32)
    result = (1.5 * side.astype(jnp.float32) - 0.5 * product).astype(jnp.bfloat16)
    return to_blocks(jnp.stack([result[:, :width], result[:, width:]], axis=0), blocks.shape[0])


def polar_real(blocks):
    values = to_matrix(blocks)
    width = values.shape[-1]
    vals = values.astype(jnp.float32)
    mean_square = jnp.sum(vals * vals, axis=(1, 2), keepdims=True) / (2 * width * width)
    scale = 0.75 / (math.sqrt(8.0 * width) * jnp.sqrt(mean_square + 1e-06))
    scaled = (vals * scale).astype(jnp.bfloat16)
    gram = jnp.einsum("nri,nrj->nij", scaled, scaled, preferred_element_type=jnp.float32).astype(
        jnp.bfloat16
    )
    product = jnp.einsum("nij,njk->nik", scaled, gram, preferred_element_type=jnp.float32)
    result = (1.5 * scaled.astype(jnp.float32) - 0.5 * product).astype(jnp.bfloat16)
    return to_blocks(result, blocks.shape[0])


def piece_widths(width):
    tiles = width // 128
    first = max(1, (tiles * 3) // 8)
    return [first * 128, width - first * 128] if tiles > 1 else [width]


def reduce_over_dp(grad_parts, own_width):
    devices_dp = lax.axis_size("dp")
    half = own_width // 2
    if devices_dp % 2 or half % 128:
        gradient = lax.psum_scatter(grad_parts[0], "dp", scatter_dimension=1, tiled=True).reshape(
            TAPS, own_width
        )
        return gradient, jnp.sum(gradient * gradient)
    d = lax.axis_index("dp")
    core = d % 2
    chip = d // 2
    chips = devices_dp // 2
    parts = grad_parts[0]
    pair = [(i, i ^ 1) for i in range(devices_dp)]
    mine, theirs, squares = [], [], []
    offset = 0
    for piece in piece_widths(half):
        keep = lax.dynamic_slice_in_dim(parts, core * half + offset, piece, axis=2)
        send = lax.dynamic_slice_in_dim(parts, (1 - core) * half + offset, piece, axis=2)
        offset += piece
        blocks = (keep + lax.ppermute(send, "dp", pair)).transpose(1, 0, 2)
        blocks = blocks.reshape(chips, 2, TAPS, piece)
        width = chips
        while width > 1:
            width //= 2
            bit = (chip // width) % 2
            split = blocks.reshape(2, width, 2, TAPS, piece)
            near = lax.dynamic_index_in_dim(split, bit, axis=0, keepdims=False)
            far = lax.dynamic_index_in_dim(split, 1 - bit, axis=0, keepdims=False)
            partner = [(i, i ^ (2 * width)) for i in range(devices_dp)]
            blocks = near + lax.ppermute(far, "dp", partner)
        blocks = blocks.reshape(2, TAPS, piece)
        squares.append(jnp.sum(blocks * blocks))
        mine.append(lax.dynamic_index_in_dim(blocks, core, axis=0, keepdims=False))
        theirs.append(
            lax.ppermute(lax.dynamic_index_in_dim(blocks, 1 - core, axis=0, keepdims=False), "dp", pair)
        )
    own = jnp.concatenate(mine, axis=1)
    other = jnp.concatenate(theirs, axis=1)
    gradient = jnp.where(
        core == 0, jnp.concatenate([own, other], axis=1), jnp.concatenate([other, own], axis=1)
    )
    return gradient, sum(squares)


def total_over_devices(value, devices):
    spread = jnp.broadcast_to(value, (devices, 1))
    gathered = lax.all_to_all(spread, AXES, 0, 0, tiled=True)
    return jnp.sum(gathered)


def on_device(grad_parts, kernel):
    devices_dp = lax.axis_size("dp")
    devices_freq = lax.axis_size("freq")
    devices = devices_dp * devices_freq
    total_freq = KD * devices
    stride = GT * GH * GW // total_freq
    scale_out = math.sqrt(C / total_freq)
    own_width = kernel.shape[1]
    rows, backward, kinds = slot_plan(total_freq, stride)

    gradient, local_square = reduce_over_dp(grad_parts, own_width)
    summed = total_over_devices(local_square, devices)
    factor = jnp.minimum(1.0, CLIP * math.sqrt(TAPS * C * C) / jnp.sqrt(summed + 1e-06))
    updated = kernel - factor * gradient

    cosine, sine = tap_phases(jnp.asarray(rows[:, 0]), stride)
    forward = jnp.where(jnp.asarray(rows[:, 1] == 0)[:, None], cosine, -sine)
    sent = jnp.einsum(
        "kpt,tf->kpf", forward.reshape(devices, 2, TAPS), updated, precision=HIGH
    ).astype(jnp.bfloat16)
    whole = lax.all_to_all(sent, AXES, 0, 0, tiled=True)

    me = lax.axis_index(AXES)
    is_pair = jnp.asarray(kinds)[me] == 1
    back = lax.cond(is_pair, polar_complex, polar_real, whole)

    returned = lax.all_to_all(back, AXES, 0, 0, tiled=True).astype(jnp.float32)
    weights = jnp.asarray(backward.reshape(TAPS, devices, 2))
    return jnp.einsum("tkp,kpf->tf", weights, returned, precision=HIGH) * scale_out


def solution(mesh):
    return jax.shard_map(
        on_device,
        mesh=mesh,
        in_specs=(P("dp", None, None, "freq"), P(None, ("dp", "freq"))),
        out_specs=P(None, ("dp", "freq")),
        check_vma=False,
    )
```

```python
import math

import numpy as np

import jax
import jax.numpy as jnp
from jax import lax
from jax.sharding import PartitionSpec as P

C = 512
TAPS = 27
GT = 8
GH = 32
GW = 32
KD = 2

CLIP = 0.25
HIGH = lax.Precision.HIGHEST
AXES = ("dp", "freq")


def grid_point(freq_ids, stride):
    flat_index = freq_ids * stride
    return flat_index // (GH * GW), flat_index // GW % GH, flat_index % GW


def turns_of(freq_ids, stride):
    freq_time, freq_row, freq_col = grid_point(freq_ids, stride)
    taps = np.arange(TAPS)
    off_time = taps // 9 - 1
    off_row = taps // 3 % 3 - 1
    off_col = taps % 3 - 1
    period = GT * GH * GW
    return (
        freq_time[:, None] * off_time[None, :] * (GH * GW)
        + freq_row[:, None] * off_row[None, :] * (GT * GW)
        + freq_col[:, None] * off_col[None, :] * (GT * GH)
    ) % period


def tap_phases(freq_ids, stride):
    flat_index = freq_ids * stride
    freq_time = flat_index // (GH * GW)
    freq_row = flat_index // GW % GH
    freq_col = flat_index % GW
    taps = jnp.arange(TAPS, dtype=jnp.int32)
    off_time = taps // 9 - 1
    off_row = taps // 3 % 3 - 1
    off_col = taps % 3 - 1
    period = GT * GH * GW
    turns = (
        freq_time[:, None] * off_time[None, :] * (GH * GW)
        + freq_row[:, None] * off_row[None, :] * (GT * GW)
        + freq_col[:, None] * off_col[None, :] * (GT * GH)
    ) % period
    angle = turns.astype(jnp.float32) * (2.0 * math.pi / period)
    return (jnp.cos(angle), jnp.sin(angle))


def slot_plan(total_freq, stride):
    ids = np.arange(total_freq)
    freq_time, freq_row, freq_col = grid_point(ids, stride)
    key = {(int(a), int(b), int(c)): j for j, (a, b, c) in enumerate(zip(freq_time, freq_row, freq_col))}
    pairs, selfs, seen = [], [], set()
    for j in range(total_freq):
        if j in seen:
            continue
        mate = key[(int(-freq_time[j] % GT), int(-freq_row[j] % GH), int(-freq_col[j] % GW))]
        seen.update((j, mate))
        if mate == j:
            selfs.append(j)
        else:
            pairs.append(j)
    assert len(selfs) % 2 == 0
    period = GT * GH * GW
    angle = turns_of(ids, stride).astype(np.float64) * (2.0 * math.pi / period)
    cosine, sine = np.cos(angle), np.sin(angle)
    forward, backward, kinds = [], [], []
    for j in pairs:
        forward += [(j, 0), (j, 1)]
        backward += [2.0 * cosine[j], -2.0 * sine[j]]
        kinds.append(1)
    for k in range(0, len(selfs), 2):
        a, b = selfs[k], selfs[k + 1]
        forward += [(a, 0), (b, 0)]
        backward += [np.round(cosine[a]), np.round(cosine[b])]
        kinds.append(0)
    forward = np.array(forward, np.int32)
    backward = np.stack(backward).T.astype(np.float32)
    return forward, backward, np.array(kinds, np.int32)


def polar_complex(values):
    width = values.shape[-1]
    vals = values.astype(jnp.float32)
    mean_square = jnp.sum(vals * vals) / (2 * width * width)
    scale = 0.75 / (math.sqrt(8.0 * width) * jnp.sqrt(mean_square + 1e-06))
    scaled = (vals * scale).astype(jnp.bfloat16)
    real_part, imag_part = scaled[0], scaled[1]
    stacked = jnp.concatenate([real_part, imag_part], axis=0)
    turned = jnp.concatenate([imag_part, -real_part], axis=0)
    gram = jnp.dot(
        stacked.T, jnp.concatenate([stacked, turned], axis=1), preferred_element_type=jnp.float32
    ).astype(jnp.bfloat16)
    gram_real = gram[:, :width]
    gram_imag = gram[:, width:]
    blocked = jnp.concatenate([gram, jnp.concatenate([-gram_imag, gram_real], axis=1)], axis=0)
    side = jnp.concatenate([real_part, imag_part], axis=1)
    product = jnp.dot(side, blocked, preferred_element_type=jnp.float32)
    result = (1.5 * side.astype(jnp.float32) - 0.5 * product).astype(jnp.bfloat16)
    return jnp.stack([result[:, :width], result[:, width:]], axis=0)


def polar_real(values):
    width = values.shape[-1]
    vals = values.astype(jnp.float32)
    mean_square = jnp.sum(vals * vals, axis=(1, 2), keepdims=True) / (2 * width * width)
    scale = 0.75 / (math.sqrt(8.0 * width) * jnp.sqrt(mean_square + 1e-06))
    scaled = (vals * scale).astype(jnp.bfloat16)
    gram = jnp.einsum("nri,nrj->nij", scaled, scaled, preferred_element_type=jnp.float32).astype(
        jnp.bfloat16
    )
    product = jnp.einsum("nij,njk->nik", scaled, gram, preferred_element_type=jnp.float32)
    return (1.5 * scaled.astype(jnp.float32) - 0.5 * product).astype(jnp.bfloat16)


def piece_widths(width):
    tiles = width // 128
    if tiles >= 8:
        first, last = (tiles * 3) // 16, tiles // 4
        return [first * 128, (tiles - first - last) * 128, last * 128]
    first = max(1, (tiles * 3) // 8)
    return [first * 128, width - first * 128] if tiles > 1 else [width]


def reduce_over_dp(grad_parts, own_width):
    devices_dp = lax.axis_size("dp")
    half = own_width // 2
    if devices_dp % 2 or half % 128:
        gradient = lax.psum_scatter(grad_parts[0], "dp", scatter_dimension=1, tiled=True).reshape(
            TAPS, own_width
        )
        return gradient, jnp.sum(gradient * gradient)
    d = lax.axis_index("dp")
    core = d % 2
    chip = d // 2
    chips = devices_dp // 2
    parts = grad_parts[0]
    pair = [(i, i ^ 1) for i in range(devices_dp)]
    mine, theirs, squares = [], [], []
    offset = 0
    for piece in piece_widths(half):
        keep = lax.dynamic_slice_in_dim(parts, core * half + offset, piece, axis=2)
        send = lax.dynamic_slice_in_dim(parts, (1 - core) * half + offset, piece, axis=2)
        offset += piece
        blocks = (keep + lax.ppermute(send, "dp", pair)).transpose(1, 0, 2)
        blocks = blocks.reshape(chips, 2, TAPS, piece)
        width = chips
        while width > 1:
            width //= 2
            bit = (chip // width) % 2
            split = blocks.reshape(2, width, 2, TAPS, piece)
            near = lax.dynamic_index_in_dim(split, bit, axis=0, keepdims=False)
            far = lax.dynamic_index_in_dim(split, 1 - bit, axis=0, keepdims=False)
            partner = [(i, i ^ (2 * width)) for i in range(devices_dp)]
            blocks = near + lax.ppermute(far, "dp", partner)
        blocks = blocks.reshape(2, TAPS, piece)
        squares.append(jnp.sum(blocks * blocks))
        mine.append(lax.dynamic_index_in_dim(blocks, core, axis=0, keepdims=False))
        theirs.append(
            lax.ppermute(lax.dynamic_index_in_dim(blocks, 1 - core, axis=0, keepdims=False), "dp", pair)
        )
    own = jnp.concatenate(mine, axis=1)
    other = jnp.concatenate(theirs, axis=1)
    gradient = jnp.where(
        core == 0, jnp.concatenate([own, other], axis=1), jnp.concatenate([other, own], axis=1)
    )
    return gradient, sum(squares)


def total_over_devices(value, devices):
    spread = jnp.broadcast_to(value, (devices, 1))
    gathered = lax.all_to_all(spread, AXES, 0, 0, tiled=True)
    return jnp.sum(gathered)


def on_device(grad_parts, kernel):
    devices_dp = lax.axis_size("dp")
    devices_freq = lax.axis_size("freq")
    devices = devices_dp * devices_freq
    total_freq = KD * devices
    stride = GT * GH * GW // total_freq
    scale_out = math.sqrt(C / total_freq)
    own_width = kernel.shape[1]
    rows, backward, kinds = slot_plan(total_freq, stride)

    gradient, local_square = reduce_over_dp(grad_parts, own_width)
    summed = total_over_devices(local_square, devices)
    factor = jnp.minimum(1.0, CLIP * math.sqrt(TAPS * C * C) / jnp.sqrt(summed + 1e-06))
    updated = kernel - factor * gradient

    cosine, sine = tap_phases(jnp.asarray(rows[:, 0]), stride)
    forward = jnp.where(jnp.asarray(rows[:, 1] == 0)[:, None], cosine, -sine)
    spectra = jnp.dot(forward, updated, precision=HIGH).astype(jnp.bfloat16)
    sent = spectra.reshape(devices, 2, own_width)
    whole = lax.all_to_all(sent, AXES, 0, 0, tiled=True)
    matrix = whole.transpose(1, 0, 2).reshape(2, C, C)

    me = lax.axis_index(AXES)
    is_pair = jnp.asarray(kinds)[me] == 1
    polar_part = lax.cond(is_pair, polar_complex, polar_real, matrix)

    back = polar_part.reshape(2, devices, own_width).transpose(1, 0, 2)
    returned = lax.all_to_all(back, AXES, 0, 0, tiled=True)
    planes = returned.reshape(2 * devices, own_width).astype(jnp.float32)
    return jnp.dot(jnp.asarray(backward), planes, precision=HIGH) * scale_out


def solution(mesh):
    return jax.shard_map(
        on_device,
        mesh=mesh,
        in_specs=(P("dp", None, None, "freq"), P(None, ("dp", "freq"))),
        out_specs=P(None, ("dp", "freq")),
        check_vma=False,
    )
```

```python
import math

import numpy as np

import jax
import jax.numpy as jnp
from jax import lax
from jax.sharding import PartitionSpec as P

C = 512
TAPS = 27
GT = 8
GH = 32
GW = 32
KD = 2

CLIP = 0.25
HIGH = lax.Precision.HIGHEST
AXES = ("dp", "freq")


def grid_point(freq_ids, stride):
    flat_index = freq_ids * stride
    return flat_index // (GH * GW), flat_index // GW % GH, flat_index % GW


def turns_of(freq_ids, stride):
    freq_time, freq_row, freq_col = grid_point(freq_ids, stride)
    taps = np.arange(TAPS)
    off_time = taps // 9 - 1
    off_row = taps // 3 % 3 - 1
    off_col = taps % 3 - 1
    period = GT * GH * GW
    return (
        freq_time[:, None] * off_time[None, :] * (GH * GW)
        + freq_row[:, None] * off_row[None, :] * (GT * GW)
        + freq_col[:, None] * off_col[None, :] * (GT * GH)
    ) % period


def tap_phases(freq_ids, stride):
    flat_index = freq_ids * stride
    freq_time = flat_index // (GH * GW)
    freq_row = flat_index // GW % GH
    freq_col = flat_index % GW
    taps = jnp.arange(TAPS, dtype=jnp.int32)
    off_time = taps // 9 - 1
    off_row = taps // 3 % 3 - 1
    off_col = taps % 3 - 1
    period = GT * GH * GW
    turns = (
        freq_time[:, None] * off_time[None, :] * (GH * GW)
        + freq_row[:, None] * off_row[None, :] * (GT * GW)
        + freq_col[:, None] * off_col[None, :] * (GT * GH)
    ) % period
    angle = turns.astype(jnp.float32) * (2.0 * math.pi / period)
    return (jnp.cos(angle), jnp.sin(angle))


def slot_plan(total_freq, stride):
    ids = np.arange(total_freq)
    freq_time, freq_row, freq_col = grid_point(ids, stride)
    key = {(int(a), int(b), int(c)): j for j, (a, b, c) in enumerate(zip(freq_time, freq_row, freq_col))}
    pairs, selfs, seen = [], [], set()
    for j in range(total_freq):
        if j in seen:
            continue
        mate = key[(int(-freq_time[j] % GT), int(-freq_row[j] % GH), int(-freq_col[j] % GW))]
        seen.update((j, mate))
        if mate == j:
            selfs.append(j)
        else:
            pairs.append(j)
    assert len(selfs) % 2 == 0
    period = GT * GH * GW
    angle = turns_of(ids, stride).astype(np.float64) * (2.0 * math.pi / period)
    cosine, sine = np.cos(angle), np.sin(angle)
    forward, backward, kinds = [], [], []
    for j in pairs:
        forward += [(j, 0), (j, 1)]
        backward += [2.0 * cosine[j], -2.0 * sine[j]]
        kinds.append(1)
    for k in range(0, len(selfs), 2):
        a, b = selfs[k], selfs[k + 1]
        forward += [(a, 0), (b, 0)]
        backward += [np.round(cosine[a]), np.round(cosine[b])]
        kinds.append(0)
    forward = np.array(forward, np.int32)
    backward = np.stack(backward).T.astype(np.float32)
    return forward, backward, np.array(kinds, np.int32)


def polar_complex(values):
    width = values.shape[-1]
    vals = values.astype(jnp.float32)
    mean_square = jnp.sum(vals * vals) / (2 * width * width)
    scale = 0.75 / (math.sqrt(8.0 * width) * jnp.sqrt(mean_square + 1e-06))
    scaled = (vals * scale).astype(jnp.bfloat16)
    real_part, imag_part = scaled[0], scaled[1]
    stacked = jnp.concatenate([real_part, imag_part], axis=0)
    turned = jnp.concatenate([imag_part, -real_part], axis=0)
    gram = jnp.dot(
        stacked.T, jnp.concatenate([stacked, turned], axis=1), preferred_element_type=jnp.float32
    ).astype(jnp.bfloat16)
    gram_real = gram[:, :width]
    gram_imag = gram[:, width:]
    blocked = jnp.concatenate([gram, jnp.concatenate([-gram_imag, gram_real], axis=1)], axis=0)
    side = jnp.concatenate([real_part, imag_part], axis=1)
    product = jnp.dot(side, blocked, preferred_element_type=jnp.float32)
    result = (1.5 * side.astype(jnp.float32) - 0.5 * product).astype(jnp.bfloat16)
    return jnp.stack([result[:, :width], result[:, width:]], axis=0)


def polar_real(values):
    width = values.shape[-1]
    vals = values.astype(jnp.float32)
    mean_square = jnp.sum(vals * vals, axis=(1, 2), keepdims=True) / (2 * width * width)
    scale = 0.75 / (math.sqrt(8.0 * width) * jnp.sqrt(mean_square + 1e-06))
    scaled = (vals * scale).astype(jnp.bfloat16)
    gram = jnp.einsum("nri,nrj->nij", scaled, scaled, preferred_element_type=jnp.float32).astype(
        jnp.bfloat16
    )
    product = jnp.einsum("nij,njk->nik", scaled, gram, preferred_element_type=jnp.float32)
    return (1.5 * scaled.astype(jnp.float32) - 0.5 * product).astype(jnp.bfloat16)


def piece_widths(width):
    tiles = width // 128
    first = max(1, tiles // 4)
    return [first * 128, width - first * 128] if tiles > 1 else [width]


def reduce_over_dp(grad_parts, own_width):
    devices_dp = lax.axis_size("dp")
    half = own_width // 2
    if devices_dp % 2 or half % 128:
        gradient = lax.psum_scatter(grad_parts[0], "dp", scatter_dimension=1, tiled=True).reshape(
            TAPS, own_width
        )
        return gradient, jnp.sum(gradient * gradient)
    d = lax.axis_index("dp")
    core = d % 2
    chip = d // 2
    chips = devices_dp // 2
    parts = grad_parts[0]
    pair = [(i, i ^ 1) for i in range(devices_dp)]
    mine, theirs, squares = [], [], []
    offset = 0
    for piece in piece_widths(half):
        keep = lax.dynamic_slice_in_dim(parts, core * half + offset, piece, axis=2)
        send = lax.dynamic_slice_in_dim(parts, (1 - core) * half + offset, piece, axis=2)
        offset += piece
        blocks = (keep + lax.ppermute(send, "dp", pair)).transpose(1, 0, 2)
        blocks = blocks.reshape(chips, 2, TAPS, piece)
        width = chips
        while width > 1:
            width //= 2
            bit = (chip // width) % 2
            split = blocks.reshape(2, width, 2, TAPS, piece)
            near = lax.dynamic_index_in_dim(split, bit, axis=0, keepdims=False)
            far = lax.dynamic_index_in_dim(split, 1 - bit, axis=0, keepdims=False)
            partner = [(i, i ^ (2 * width)) for i in range(devices_dp)]
            blocks = near + lax.ppermute(far, "dp", partner)
        blocks = blocks.reshape(2, TAPS, piece)
        squares.append(jnp.sum(blocks * blocks))
        mine.append(lax.dynamic_index_in_dim(blocks, core, axis=0, keepdims=False))
        theirs.append(
            lax.ppermute(lax.dynamic_index_in_dim(blocks, 1 - core, axis=0, keepdims=False), "dp", pair)
        )
    own = jnp.concatenate(mine, axis=1)
    other = jnp.concatenate(theirs, axis=1)
    gradient = jnp.where(
        core == 0, jnp.concatenate([own, other], axis=1), jnp.concatenate([other, own], axis=1)
    )
    return gradient, sum(squares)


def total_over_devices(value, devices):
    spread = jnp.broadcast_to(value, (devices, 1))
    gathered = lax.all_to_all(spread, AXES, 0, 0, tiled=True)
    return jnp.sum(gathered)


def on_device(grad_parts, kernel):
    devices_dp = lax.axis_size("dp")
    devices_freq = lax.axis_size("freq")
    devices = devices_dp * devices_freq
    total_freq = KD * devices
    stride = GT * GH * GW // total_freq
    scale_out = math.sqrt(C / total_freq)
    own_width = kernel.shape[1]
    rows, backward, kinds = slot_plan(total_freq, stride)

    gradient, local_square = reduce_over_dp(grad_parts, own_width)
    summed = total_over_devices(local_square, devices)
    factor = jnp.minimum(1.0, CLIP * math.sqrt(TAPS * C * C) / jnp.sqrt(summed + 1e-06))
    updated = kernel - factor * gradient

    cosine, sine = tap_phases(jnp.asarray(rows[:, 0]), stride)
    forward = jnp.where(jnp.asarray(rows[:, 1] == 0)[:, None], cosine, -sine)
    spectra = jnp.dot(forward, updated, precision=HIGH).astype(jnp.bfloat16)
    sent = spectra.reshape(devices, 2, own_width)
    whole = lax.all_to_all(sent, AXES, 0, 0, tiled=True)
    matrix = whole.transpose(1, 0, 2).reshape(2, C, C)

    me = lax.axis_index(AXES)
    is_pair = jnp.asarray(kinds)[me] == 1
    polar_part = lax.cond(is_pair, polar_complex, polar_real, matrix)

    back = polar_part.reshape(2, devices, own_width).transpose(1, 0, 2)
    returned = lax.all_to_all(back, AXES, 0, 0, tiled=True)
    planes = returned.reshape(2 * devices, own_width).astype(jnp.float32)
    return jnp.dot(jnp.asarray(backward), planes, precision=HIGH) * scale_out


def solution(mesh):
    return jax.shard_map(
        on_device,
        mesh=mesh,
        in_specs=(P("dp", None, None, "freq"), P(None, ("dp", "freq"))),
        out_specs=P(None, ("dp", "freq")),
        check_vma=False,
    )
```

```python
import math

import numpy as np

import jax
import jax.numpy as jnp
from jax import lax
from jax.sharding import PartitionSpec as P

C = 512
TAPS = 27
GT = 8
GH = 32
GW = 32
KD = 2

CLIP = 0.25
HIGH = lax.Precision.HIGHEST
AXES = ("dp", "freq")


def grid_point(freq_ids, stride):
    flat_index = freq_ids * stride
    return flat_index // (GH * GW), flat_index // GW % GH, flat_index % GW


def turns_of(freq_ids, stride):
    freq_time, freq_row, freq_col = grid_point(freq_ids, stride)
    taps = np.arange(TAPS)
    off_time = taps // 9 - 1
    off_row = taps // 3 % 3 - 1
    off_col = taps % 3 - 1
    period = GT * GH * GW
    return (
        freq_time[:, None] * off_time[None, :] * (GH * GW)
        + freq_row[:, None] * off_row[None, :] * (GT * GW)
        + freq_col[:, None] * off_col[None, :] * (GT * GH)
    ) % period


def tap_phases(freq_ids, stride):
    flat_index = freq_ids * stride
    freq_time = flat_index // (GH * GW)
    freq_row = flat_index // GW % GH
    freq_col = flat_index % GW
    taps = jnp.arange(TAPS, dtype=jnp.int32)
    off_time = taps // 9 - 1
    off_row = taps // 3 % 3 - 1
    off_col = taps % 3 - 1
    period = GT * GH * GW
    turns = (
        freq_time[:, None] * off_time[None, :] * (GH * GW)
        + freq_row[:, None] * off_row[None, :] * (GT * GW)
        + freq_col[:, None] * off_col[None, :] * (GT * GH)
    ) % period
    angle = turns.astype(jnp.float32) * (2.0 * math.pi / period)
    return (jnp.cos(angle), jnp.sin(angle))


def slot_plan(total_freq, stride):
    ids = np.arange(total_freq)
    freq_time, freq_row, freq_col = grid_point(ids, stride)
    key = {(int(a), int(b), int(c)): j for j, (a, b, c) in enumerate(zip(freq_time, freq_row, freq_col))}
    pairs, selfs, seen = [], [], set()
    for j in range(total_freq):
        if j in seen:
            continue
        mate = key[(int(-freq_time[j] % GT), int(-freq_row[j] % GH), int(-freq_col[j] % GW))]
        seen.update((j, mate))
        if mate == j:
            selfs.append(j)
        else:
            pairs.append(j)
    assert len(selfs) % 2 == 0
    period = GT * GH * GW
    angle = turns_of(ids, stride).astype(np.float64) * (2.0 * math.pi / period)
    cosine, sine = np.cos(angle), np.sin(angle)
    forward, backward, kinds = [], [], []
    for j in pairs:
        forward += [(j, 0), (j, 1)]
        backward += [2.0 * cosine[j], -2.0 * sine[j]]
        kinds.append(1)
    for k in range(0, len(selfs), 2):
        a, b = selfs[k], selfs[k + 1]
        forward += [(a, 0), (b, 0)]
        backward += [np.round(cosine[a]), np.round(cosine[b])]
        kinds.append(0)
    forward = np.array(forward, np.int32)
    backward = np.stack(backward).T.astype(np.float32)
    return forward, backward, np.array(kinds, np.int32)


def polar_complex(values):
    width = values.shape[-1]
    vals = values.astype(jnp.float32)
    mean_square = jnp.sum(vals * vals) / (2 * width * width)
    scale = 0.75 / (math.sqrt(8.0 * width) * jnp.sqrt(mean_square + 1e-06))
    scaled = (vals * scale).astype(jnp.bfloat16)
    real_part, imag_part = scaled[0], scaled[1]
    stacked = jnp.concatenate([real_part, imag_part], axis=0)
    turned = jnp.concatenate([imag_part, -real_part], axis=0)
    gram = jnp.dot(
        stacked.T, jnp.concatenate([stacked, turned], axis=1), preferred_element_type=jnp.float32
    ).astype(jnp.bfloat16)
    gram_real = gram[:, :width]
    gram_imag = gram[:, width:]
    blocked = jnp.concatenate([gram, jnp.concatenate([-gram_imag, gram_real], axis=1)], axis=0)
    side = jnp.concatenate([real_part, imag_part], axis=1)
    product = jnp.dot(side, blocked, preferred_element_type=jnp.float32)
    result = (1.5 * side.astype(jnp.float32) - 0.5 * product).astype(jnp.bfloat16)
    return jnp.stack([result[:, :width], result[:, width:]], axis=0)


def polar_real(values):
    width = values.shape[-1]
    vals = values.astype(jnp.float32)
    mean_square = jnp.sum(vals * vals, axis=(1, 2), keepdims=True) / (2 * width * width)
    scale = 0.75 / (math.sqrt(8.0 * width) * jnp.sqrt(mean_square + 1e-06))
    scaled = (vals * scale).astype(jnp.bfloat16)
    gram = jnp.einsum("nri,nrj->nij", scaled, scaled, preferred_element_type=jnp.float32).astype(
        jnp.bfloat16
    )
    product = jnp.einsum("nij,njk->nik", scaled, gram, preferred_element_type=jnp.float32)
    return (1.5 * scaled.astype(jnp.float32) - 0.5 * product).astype(jnp.bfloat16)


def piece_widths(width):
    tiles = width // 128
    first = max(1, (tiles * 3) // 8)
    return [first * 128, width - first * 128] if tiles > 1 else [width]


def reduce_over_dp(grad_parts, own_width):
    devices_dp = lax.axis_size("dp")
    half = own_width // 2
    if devices_dp % 2 or half % 128:
        gradient = lax.psum_scatter(grad_parts[0], "dp", scatter_dimension=1, tiled=True).reshape(
            TAPS, own_width
        )
        return gradient, jnp.sum(gradient * gradient)
    d = lax.axis_index("dp")
    core = d % 2
    chip = d // 2
    chips = devices_dp // 2
    parts = grad_parts[0]
    pair = [(i, i ^ 1) for i in range(devices_dp)]
    mine, theirs, squares = [], [], []
    offset = 0
    for piece in piece_widths(half):
        keep = lax.dynamic_slice_in_dim(parts, core * half + offset, piece, axis=2)
        send = lax.dynamic_slice_in_dim(parts, (1 - core) * half + offset, piece, axis=2)
        offset += piece
        blocks = (keep + lax.ppermute(send, "dp", pair)).transpose(1, 0, 2)
        blocks = blocks.reshape(chips, 2, TAPS, piece)
        width = chips
        while width > 1:
            width //= 2
            bit = (chip // width) % 2
            split = blocks.reshape(2, width, 2, TAPS, piece)
            near = lax.dynamic_index_in_dim(split, bit, axis=0, keepdims=False)
            far = lax.dynamic_index_in_dim(split, 1 - bit, axis=0, keepdims=False)
            partner = [(i, i ^ (2 * width)) for i in range(devices_dp)]
            blocks = near + lax.ppermute(far, "dp", partner)
        blocks = blocks.reshape(2, TAPS, piece)
        squares.append(jnp.sum(lax.optimization_barrier(jnp.sum(blocks * blocks, axis=(0, 1)))))
        mine.append(lax.dynamic_index_in_dim(blocks, core, axis=0, keepdims=False))
        theirs.append(
            lax.ppermute(lax.dynamic_index_in_dim(blocks, 1 - core, axis=0, keepdims=False), "dp", pair)
        )
    own = jnp.concatenate(mine, axis=1)
    other = jnp.concatenate(theirs, axis=1)
    gradient = jnp.where(
        core == 0, jnp.concatenate([own, other], axis=1), jnp.concatenate([other, own], axis=1)
    )
    return gradient, sum(squares)


def total_over_devices(value, devices):
    spread = jnp.broadcast_to(value, (devices, 1))
    gathered = lax.all_to_all(spread, AXES, 0, 0, tiled=True)
    return jnp.sum(gathered)


def on_device(grad_parts, kernel):
    devices_dp = lax.axis_size("dp")
    devices_freq = lax.axis_size("freq")
    devices = devices_dp * devices_freq
    total_freq = KD * devices
    stride = GT * GH * GW // total_freq
    scale_out = math.sqrt(C / total_freq)
    own_width = kernel.shape[1]
    rows, backward, kinds = slot_plan(total_freq, stride)

    gradient, local_square = reduce_over_dp(grad_parts, own_width)
    summed = total_over_devices(local_square, devices)
    factor = jnp.minimum(1.0, CLIP * math.sqrt(TAPS * C * C) / jnp.sqrt(summed + 1e-06))
    updated = kernel - factor * gradient

    cosine, sine = tap_phases(jnp.asarray(rows[:, 0]), stride)
    forward = jnp.where(jnp.asarray(rows[:, 1] == 0)[:, None], cosine, -sine)
    spectra = jnp.dot(forward, updated, precision=HIGH).astype(jnp.bfloat16)
    sent = spectra.reshape(devices, 2, own_width)
    whole = lax.all_to_all(sent, AXES, 0, 0, tiled=True)
    matrix = whole.transpose(1, 0, 2).reshape(2, C, C)

    me = lax.axis_index(AXES)
    is_pair = jnp.asarray(kinds)[me] == 1
    polar_part = lax.cond(is_pair, polar_complex, polar_real, matrix)

    back = polar_part.reshape(2, devices, own_width).transpose(1, 0, 2)
    returned = lax.all_to_all(back, AXES, 0, 0, tiled=True)
    planes = returned.reshape(2 * devices, own_width).astype(jnp.float32)
    return jnp.dot(jnp.asarray(backward), planes, precision=HIGH) * scale_out


def solution(mesh):
    return jax.shard_map(
        on_device,
        mesh=mesh,
        in_specs=(P("dp", None, None, "freq"), P(None, ("dp", "freq"))),
        out_specs=P(None, ("dp", "freq")),
        check_vma=False,
    )
```

```python
import math

import numpy as np

import jax
import jax.numpy as jnp
from jax import lax
from jax.sharding import PartitionSpec as P

C = 512
TAPS = 27
GT = 8
GH = 32
GW = 32
KD = 2

CLIP = 0.25
HIGH = lax.Precision.HIGHEST
AXES = ("dp", "freq")


def grid_point(freq_ids, stride):
    flat_index = freq_ids * stride
    return flat_index // (GH * GW), flat_index // GW % GH, flat_index % GW


def turns_of(freq_ids, stride):
    freq_time, freq_row, freq_col = grid_point(freq_ids, stride)
    taps = np.arange(TAPS)
    off_time = taps // 9 - 1
    off_row = taps // 3 % 3 - 1
    off_col = taps % 3 - 1
    period = GT * GH * GW
    return (
        freq_time[:, None] * off_time[None, :] * (GH * GW)
        + freq_row[:, None] * off_row[None, :] * (GT * GW)
        + freq_col[:, None] * off_col[None, :] * (GT * GH)
    ) % period


def tap_phases(freq_ids, stride):
    flat_index = freq_ids * stride
    freq_time = flat_index // (GH * GW)
    freq_row = flat_index // GW % GH
    freq_col = flat_index % GW
    taps = jnp.arange(TAPS, dtype=jnp.int32)
    off_time = taps // 9 - 1
    off_row = taps // 3 % 3 - 1
    off_col = taps % 3 - 1
    period = GT * GH * GW
    turns = (
        freq_time[:, None] * off_time[None, :] * (GH * GW)
        + freq_row[:, None] * off_row[None, :] * (GT * GW)
        + freq_col[:, None] * off_col[None, :] * (GT * GH)
    ) % period
    angle = turns.astype(jnp.float32) * (2.0 * math.pi / period)
    return (jnp.cos(angle), jnp.sin(angle))


def slot_plan(total_freq, stride):
    ids = np.arange(total_freq)
    freq_time, freq_row, freq_col = grid_point(ids, stride)
    key = {(int(a), int(b), int(c)): j for j, (a, b, c) in enumerate(zip(freq_time, freq_row, freq_col))}
    pairs, selfs, seen = [], [], set()
    for j in range(total_freq):
        if j in seen:
            continue
        mate = key[(int(-freq_time[j] % GT), int(-freq_row[j] % GH), int(-freq_col[j] % GW))]
        seen.update((j, mate))
        if mate == j:
            selfs.append(j)
        else:
            pairs.append(j)
    assert len(selfs) % 2 == 0
    period = GT * GH * GW
    angle = turns_of(ids, stride).astype(np.float64) * (2.0 * math.pi / period)
    cosine, sine = np.cos(angle), np.sin(angle)
    forward, backward, kinds = [], [], []
    for j in pairs:
        forward += [(j, 0), (j, 1)]
        backward += [2.0 * cosine[j], -2.0 * sine[j]]
        kinds.append(1)
    for k in range(0, len(selfs), 2):
        a, b = selfs[k], selfs[k + 1]
        forward += [(a, 0), (b, 0)]
        backward += [np.round(cosine[a]), np.round(cosine[b])]
        kinds.append(0)
    forward = np.array(forward, np.int32)
    backward = np.stack(backward).T.astype(np.float32)
    return forward, backward, np.array(kinds, np.int32)


def polar_complex(values):
    width = values.shape[-1]
    vals = values.astype(jnp.float32)
    mean_square = jnp.sum(vals * vals) / (2 * width * width)
    scale = 0.75 / (math.sqrt(8.0 * width) * jnp.sqrt(mean_square + 1e-06))
    scaled = (vals * scale).astype(jnp.bfloat16)
    real_part, imag_part = scaled[0], scaled[1]
    stacked = jnp.concatenate([real_part, imag_part], axis=0)
    turned = jnp.concatenate([imag_part, -real_part], axis=0)
    gram = jnp.dot(
        stacked.T, jnp.concatenate([stacked, turned], axis=1), preferred_element_type=jnp.float32
    ).astype(jnp.bfloat16)
    gram_real = gram[:, :width]
    gram_imag = gram[:, width:]
    blocked = jnp.concatenate([gram, jnp.concatenate([-gram_imag, gram_real], axis=1)], axis=0)
    side = jnp.concatenate([real_part, imag_part], axis=1)
    product = jnp.dot(side, blocked, preferred_element_type=jnp.float32)
    result = (1.5 * side.astype(jnp.float32) - 0.5 * product).astype(jnp.bfloat16)
    return jnp.stack([result[:, :width], result[:, width:]], axis=0)


def polar_real(values):
    width = values.shape[-1]
    vals = values.astype(jnp.float32)
    mean_square = jnp.sum(vals * vals, axis=(1, 2), keepdims=True) / (2 * width * width)
    scale = 0.75 / (math.sqrt(8.0 * width) * jnp.sqrt(mean_square + 1e-06))
    scaled = (vals * scale).astype(jnp.bfloat16)
    gram = jnp.einsum("nri,nrj->nij", scaled, scaled, preferred_element_type=jnp.float32).astype(
        jnp.bfloat16
    )
    product = jnp.einsum("nij,njk->nik", scaled, gram, preferred_element_type=jnp.float32)
    return (1.5 * scaled.astype(jnp.float32) - 0.5 * product).astype(jnp.bfloat16)


def piece_widths(width):
    tiles = width // 128
    first = max(1, (tiles * 3) // 8)
    return [first * 128, width - first * 128] if tiles > 1 else [width]


def reduce_over_dp(grad_parts, own_width):
    devices_dp = lax.axis_size("dp")
    half = own_width // 2
    if devices_dp % 2 or half % 128:
        gradient = lax.psum_scatter(grad_parts[0], "dp", scatter_dimension=1, tiled=True).reshape(
            TAPS, own_width
        )
        return gradient, jnp.sum(gradient * gradient)
    d = lax.axis_index("dp")
    core = d % 2
    chip = d // 2
    chips = devices_dp // 2
    parts = grad_parts[0]
    pair = [(i, i ^ 1) for i in range(devices_dp)]
    mine, theirs, squares = [], [], []
    offset = 0
    for piece in piece_widths(half):
        keep = lax.dynamic_slice_in_dim(parts, core * half + offset, piece, axis=2)
        send = lax.dynamic_slice_in_dim(parts, (1 - core) * half + offset, piece, axis=2)
        offset += piece
        blocks = (keep + lax.ppermute(send, "dp", pair)).transpose(1, 0, 2)
        blocks = blocks.reshape(chips, 2, TAPS, piece)
        width = chips
        while width > 1:
            width //= 2
            bit = (chip // width) % 2
            split = blocks.reshape(2, width, 2, TAPS, piece)
            near = lax.dynamic_index_in_dim(split, bit, axis=0, keepdims=False)
            far = lax.dynamic_index_in_dim(split, 1 - bit, axis=0, keepdims=False)
            partner = [(i, i ^ (2 * width)) for i in range(devices_dp)]
            blocks = near + lax.ppermute(far, "dp", partner)
        blocks = blocks.reshape(2, TAPS, piece)
        squares.append(jnp.sum(blocks * blocks))
        mine.append(lax.dynamic_index_in_dim(blocks, core, axis=0, keepdims=False))
        theirs.append(
            lax.ppermute(lax.dynamic_index_in_dim(blocks, 1 - core, axis=0, keepdims=False), "dp", pair)
        )
    own = jnp.concatenate(mine, axis=1)
    other = jnp.concatenate(theirs, axis=1)
    gradient = jnp.where(
        core == 0, jnp.concatenate([own, other], axis=1), jnp.concatenate([other, own], axis=1)
    )
    return gradient, sum(squares)


def total_over_devices(value, devices):
    spread = jnp.broadcast_to(value, (devices, 1))
    gathered = lax.all_to_all(spread, AXES, 0, 0, tiled=True)
    return jnp.sum(gathered)


def on_device(grad_parts, kernel):
    devices_dp = lax.axis_size("dp")
    devices_freq = lax.axis_size("freq")
    devices = devices_dp * devices_freq
    total_freq = KD * devices
    stride = GT * GH * GW // total_freq
    scale_out = math.sqrt(C / total_freq)
    own_width = kernel.shape[1]
    rows, backward, kinds = slot_plan(total_freq, stride)

    gradient, local_square = reduce_over_dp(grad_parts, own_width)
    summed = total_over_devices(local_square, devices)
    factor = jnp.minimum(1.0, CLIP * math.sqrt(TAPS * C * C) / jnp.sqrt(summed + 1e-06))
    updated = kernel - factor * gradient

    cosine, sine = tap_phases(jnp.asarray(rows[:, 0]), stride)
    forward = jnp.where(jnp.asarray(rows[:, 1] == 0)[:, None], cosine, -sine)
    spectra = jnp.dot(forward, updated, precision=HIGH).astype(jnp.bfloat16)
    rows_each = own_width // C
    sent = spectra.reshape(devices, 2, rows_each, C)
    whole = lax.all_to_all(sent, AXES, 0, 0, tiled=True)
    matrix = whole.transpose(1, 0, 2, 3).reshape(2, C, C)

    me = lax.axis_index(AXES)
    is_pair = jnp.asarray(kinds)[me] == 1
    polar_part = lax.cond(is_pair, polar_complex, polar_real, matrix)

    back = polar_part.reshape(2, devices, rows_each, C).transpose(1, 0, 2, 3)
    returned = lax.all_to_all(back, AXES, 0, 0, tiled=True)
    planes = returned.reshape(2 * devices, own_width).astype(jnp.float32)
    return jnp.dot(jnp.asarray(backward), planes, precision=HIGH) * scale_out


def solution(mesh):
    return jax.shard_map(
        on_device,
        mesh=mesh,
        in_specs=(P("dp", None, None, "freq"), P(None, ("dp", "freq"))),
        out_specs=P(None, ("dp", "freq")),
        check_vma=False,
    )
```

```python
import math

import numpy as np

import jax
import jax.numpy as jnp
from jax import lax
from jax.sharding import PartitionSpec as P

C = 512
TAPS = 27
GT = 8
GH = 32
GW = 32
KD = 2

CLIP = 0.25
HIGH = lax.Precision.HIGHEST
AXES = ("dp", "freq")


def grid_point(freq_ids, stride):
    flat_index = freq_ids * stride
    return flat_index // (GH * GW), flat_index // GW % GH, flat_index % GW


def turns_of(freq_ids, stride):
    freq_time, freq_row, freq_col = grid_point(freq_ids, stride)
    taps = np.arange(TAPS)
    off_time = taps // 9 - 1
    off_row = taps // 3 % 3 - 1
    off_col = taps % 3 - 1
    period = GT * GH * GW
    return (
        freq_time[:, None] * off_time[None, :] * (GH * GW)
        + freq_row[:, None] * off_row[None, :] * (GT * GW)
        + freq_col[:, None] * off_col[None, :] * (GT * GH)
    ) % period


def tap_phases(freq_ids, stride):
    flat_index = freq_ids * stride
    freq_time = flat_index // (GH * GW)
    freq_row = flat_index // GW % GH
    freq_col = flat_index % GW
    taps = jnp.arange(TAPS, dtype=jnp.int32)
    off_time = taps // 9 - 1
    off_row = taps // 3 % 3 - 1
    off_col = taps % 3 - 1
    period = GT * GH * GW
    turns = (
        freq_time[:, None] * off_time[None, :] * (GH * GW)
        + freq_row[:, None] * off_row[None, :] * (GT * GW)
        + freq_col[:, None] * off_col[None, :] * (GT * GH)
    ) % period
    angle = turns.astype(jnp.float32) * (2.0 * math.pi / period)
    return (jnp.cos(angle), jnp.sin(angle))


def slot_plan(total_freq, stride):
    ids = np.arange(total_freq)
    freq_time, freq_row, freq_col = grid_point(ids, stride)
    key = {(int(a), int(b), int(c)): j for j, (a, b, c) in enumerate(zip(freq_time, freq_row, freq_col))}
    pairs, selfs, seen = [], [], set()
    for j in range(total_freq):
        if j in seen:
            continue
        mate = key[(int(-freq_time[j] % GT), int(-freq_row[j] % GH), int(-freq_col[j] % GW))]
        seen.update((j, mate))
        if mate == j:
            selfs.append(j)
        else:
            pairs.append(j)
    assert len(selfs) % 2 == 0
    period = GT * GH * GW
    angle = turns_of(ids, stride).astype(np.float64) * (2.0 * math.pi / period)
    cosine, sine = np.cos(angle), np.sin(angle)
    forward, backward, kinds = [], [], []
    for j in pairs:
        forward += [(j, 0), (j, 1)]
        backward += [2.0 * cosine[j], -2.0 * sine[j]]
        kinds.append(1)
    for k in range(0, len(selfs), 2):
        a, b = selfs[k], selfs[k + 1]
        forward += [(a, 0), (b, 0)]
        backward += [np.round(cosine[a]), np.round(cosine[b])]
        kinds.append(0)
    forward = np.array(forward, np.int32)
    backward = np.stack(backward).T.astype(np.float32)
    return forward, backward, np.array(kinds, np.int32)


def polar_complex(values):
    width = values.shape[-1]
    vals = values.astype(jnp.float32)
    mean_square = jnp.sum(vals * vals) / (2 * width * width)
    scale = 0.75 / (math.sqrt(8.0 * width) * jnp.sqrt(mean_square + 1e-06))
    scaled = (vals * scale).astype(jnp.bfloat16)
    real_part, imag_part = scaled[0], scaled[1]
    stacked = jnp.concatenate([real_part, imag_part], axis=0)
    turned = jnp.concatenate([imag_part, -real_part], axis=0)
    gram = jnp.dot(
        stacked.T, jnp.concatenate([stacked, turned], axis=1), preferred_element_type=jnp.float32
    ).astype(jnp.bfloat16)
    gram_real = gram[:, :width]
    gram_imag = gram[:, width:]
    blocked = jnp.concatenate([gram, jnp.concatenate([-gram_imag, gram_real], axis=1)], axis=0)
    side = jnp.concatenate([real_part, imag_part], axis=1)
    product = jnp.dot(side, blocked, preferred_element_type=jnp.float32)
    result = (1.5 * side.astype(jnp.float32) - 0.5 * product).astype(jnp.bfloat16)
    return jnp.stack([result[:, :width], result[:, width:]], axis=0)


def polar_real(values):
    width = values.shape[-1]
    vals = values.astype(jnp.float32)
    mean_square = jnp.sum(vals * vals, axis=(1, 2), keepdims=True) / (2 * width * width)
    scale = 0.75 / (math.sqrt(8.0 * width) * jnp.sqrt(mean_square + 1e-06))
    scaled = (vals * scale).astype(jnp.bfloat16)
    gram = jnp.einsum("nri,nrj->nij", scaled, scaled, preferred_element_type=jnp.float32).astype(
        jnp.bfloat16
    )
    product = jnp.einsum("nij,njk->nik", scaled, gram, preferred_element_type=jnp.float32)
    return (1.5 * scaled.astype(jnp.float32) - 0.5 * product).astype(jnp.bfloat16)


def piece_widths(width):
    tiles = width // 128
    first = max(1, (tiles * 3) // 8)
    return [first * 128, width - first * 128] if tiles > 1 else [width]


def reduce_over_dp(grad_parts, own_width):
    devices_dp = lax.axis_size("dp")
    half = own_width // 2
    if devices_dp % 2 or half % 128:
        gradient = lax.psum_scatter(grad_parts[0], "dp", scatter_dimension=1, tiled=True).reshape(
            TAPS, own_width
        )
        return gradient, jnp.sum(gradient * gradient)
    d = lax.axis_index("dp")
    core = d % 2
    chip = d // 2
    chips = devices_dp // 2
    parts = grad_parts[0]
    pair = [(i, i ^ 1) for i in range(devices_dp)]
    mine, theirs, squares = [], [], []
    offset = 0
    for piece in piece_widths(half):
        keep = lax.dynamic_slice_in_dim(parts, core * half + offset, piece, axis=2)
        send = lax.dynamic_slice_in_dim(parts, (1 - core) * half + offset, piece, axis=2)
        offset += piece
        blocks = (keep + lax.ppermute(send, "dp", pair)).transpose(1, 0, 2)
        blocks = blocks.reshape(chips, 2, TAPS, piece)
        width = chips
        while width > 1:
            width //= 2
            bit = (chip // width) % 2
            split = blocks.reshape(2, width, 2, TAPS, piece)
            near = lax.dynamic_index_in_dim(split, bit, axis=0, keepdims=False)
            far = lax.dynamic_index_in_dim(split, 1 - bit, axis=0, keepdims=False)
            partner = [(i, i ^ (2 * width)) for i in range(devices_dp)]
            blocks = near + lax.ppermute(far, "dp", partner)
        blocks = blocks.reshape(2, TAPS, piece)
        squares.append(jnp.sum(blocks * blocks))
        mine.append(lax.dynamic_index_in_dim(blocks, core, axis=0, keepdims=False))
        theirs.append(
            lax.ppermute(lax.dynamic_index_in_dim(blocks, 1 - core, axis=0, keepdims=False), "dp", pair)
        )
    own = jnp.concatenate(mine, axis=1)
    other = jnp.concatenate(theirs, axis=1)
    gradient = jnp.where(
        core == 0, jnp.concatenate([own, other], axis=1), jnp.concatenate([other, own], axis=1)
    )
    return gradient, sum(squares)


def total_over_devices(value, devices):
    spread = jnp.broadcast_to(value, (devices, 1))
    gathered = lax.all_to_all(spread, AXES, 0, 0, tiled=True)
    return jnp.sum(gathered)


def on_device(grad_parts, kernel):
    devices_dp = lax.axis_size("dp")
    devices_freq = lax.axis_size("freq")
    devices = devices_dp * devices_freq
    total_freq = KD * devices
    stride = GT * GH * GW // total_freq
    scale_out = math.sqrt(C / total_freq)
    own_width = kernel.shape[1]
    rows, backward, kinds = slot_plan(total_freq, stride)

    gradient, local_square = reduce_over_dp(grad_parts, own_width)
    summed = total_over_devices(local_square, devices)
    factor = jnp.minimum(1.0, CLIP * math.sqrt(TAPS * C * C) / jnp.sqrt(summed + 1e-06))
    updated = kernel - factor * gradient

    cosine, sine = tap_phases(jnp.asarray(rows[:, 0]), stride)
    forward = jnp.where(jnp.asarray(rows[:, 1] == 0)[:, None], cosine, -sine)
    spectra = jnp.dot(forward, updated, precision=HIGH).astype(jnp.bfloat16)
    rows_each = own_width // C
    sent = spectra.reshape(devices, 2, rows_each, C)
    whole = lax.all_to_all(sent, AXES, 0, 0, tiled=True)

    me = lax.axis_index(AXES)
    is_pair = jnp.asarray(kinds)[me] == 1

    def in_blocks(polar):
        def step(blocks):
            matrix = blocks.transpose(1, 0, 2, 3).reshape(2, C, C)
            return polar(matrix).reshape(2, devices, rows_each, C).transpose(1, 0, 2, 3)

        return step

    back = lax.cond(is_pair, in_blocks(polar_complex), in_blocks(polar_real), whole)
    returned = lax.all_to_all(back, AXES, 0, 0, tiled=True)
    planes = returned.reshape(2 * devices, own_width).astype(jnp.float32)
    return jnp.dot(jnp.asarray(backward), planes, precision=HIGH) * scale_out


def solution(mesh):
    return jax.shard_map(
        on_device,
        mesh=mesh,
        in_specs=(P("dp", None, None, "freq"), P(None, ("dp", "freq"))),
        out_specs=P(None, ("dp", "freq")),
        check_vma=False,
    )
```
